128 devices in a mesh: fsdp: 8 (over x, core), dp: 16 (over z, y).
Axes of the slice: x: 4, y: 4, z: 4, core: 2. Of those that a mesh axis runs over, the one named last changes fastest.
Arguments:
- patch_states: bfloat16 [131072, 1280], P(('fsdp', 'dp')), may hold values from -6 to 6
- segment_ids: int32 [131072], P(('fsdp', 'dp')), may hold values from 0 to 63, as said below
- first_gain: float32 [1280], replicated, may hold values from 0.1 to 1.9
- first_shift: float32 [1280], replicated, may hold values from -3 to 3
- qkv_weight: bfloat16 [3840, 1280], P(('fsdp', 'dp')), may hold values from -1.5 to 1.5
- qkv_bias: float32 [3840], replicated, may hold values from -3 to 3
- out_weight: bfloat16 [1280, 1280], P(('fsdp', 'dp')), may hold values from -0.15625 to 0.15625
- out_bias: float32 [1280], replicated, may hold values from -3 to 3
- second_gain: float32 [1280], replicated, may hold values from 0.1 to 1.9
- second_shift: float32 [1280], replicated, may hold values from -3 to 3
- merge_weight: bfloat16 [1280, 5120], P(('fsdp', 'dp')), may hold values from -0.078125 to 0.078125
- merge_bias: float32 [1280], replicated, may hold values from -3 to 3
- dest_device: int32 [32768], P(('fsdp', 'dp')), may hold values from 0 to 127, as said below
- dest_slot: int32 [32768], P(('fsdp', 'dp')), may hold values from 0 to 255, as said below
Outputs:
- requests: bfloat16 [32768, 1280], P(('fsdp', 'dp'))
The draws below stay inside these ranges and needn't reach their ends.
Inputs may be any that keep to these rules, and one draw needn't show every extreme that they name: `segment_ids`: within each device's 1024 tokens the ids start at 0, never fall, and change only between aligned groups of 4 tokens. `dest_device`: every device receives exactly 256 merged rows; the rows from one device to one device number 0, 2 or 4, and 4 for some pairs. The pairs of dest_device and dest_slot are all different.
All inputs are finite; a program needn't handle non-finite values.
Results may differ from the reference program's by a relative error of at most 0.0062.
Values may be sent and summed in bfloat16 or wider, within the bound.
No kernel may reach another device: no remote copies, remote signals or barrier semaphores. Data moves between devices by JAX's collectives and lax.ppermute only.
A program may use at most 128 MiB of HBM per device.

```python
import math
import jax
import jax.numpy as jnp
from jax import lax

D = 1280
H = 16
HD = 80
TOK_DEV = 1024
TOKENS = 131072
MROWS = 256
MERGED = 32768


def draw_patch_states(key, part):
    keys = jax.random.split(key, 3)
    base = jnp.clip(jax.random.normal(keys[0], (TOKENS, D), jnp.float32), -6.0, 6.0)
    column = 0.1 * jnp.exp(jax.random.uniform(keys[1], (D,), jnp.float32) * math.log(10.0))
    rowscale = 0.1 * jnp.exp(jax.random.uniform(keys[2], (TOKENS,), jnp.float32) * math.log(10.0))
    return (base * column[None, :] * rowscale[:, None]).astype(jnp.bfloat16)


def draw_qkv_weight(key, part):
    normal_part = jnp.clip(jax.random.normal(key, (3, D, D), jnp.float32), -6.0, 6.0) / math.sqrt(D)
    whole = normal_part.reshape(3 * D, D)
    return jnp.clip(whole, -1.5, 1.5).astype(jnp.bfloat16)


def draw_segment_ids(key, part):
    packed = TOKENS // TOK_DEV
    windows = TOK_DEV // 4
    most_id = windows // 4 - 1
    first, second, third = jax.random.split(key, 3)
    level = jax.random.randint(first, (packed,), 0, 4)
    threshold = jnp.array([0, 1, 2, 4], jnp.int32)[level]
    draws = jax.random.randint(second, (packed, windows), 0, 64)
    breaks = (draws < threshold[:, None]).astype(jnp.int32)
    busiest = jax.random.randint(third, (), 0, packed)
    window_index = jnp.arange(windows, dtype=jnp.int32)
    forced = (window_index % 4 == 0).astype(jnp.int32)
    is_busiest = (jnp.arange(packed, dtype=jnp.int32) == busiest)[:, None]
    breaks = jnp.where(is_busiest, forced[None, :], breaks)
    breaks = breaks.at[:, 0].set(0)
    window_ids = jnp.minimum(jnp.cumsum(breaks, axis=1), most_id).astype(jnp.int32)
    return jnp.repeat(window_ids, 4, axis=1).reshape(TOKENS).astype(jnp.int32)


def routing_tables(key):
    base_key = jax.random.fold_in(key, 11)
    keys = jax.random.split(base_key, 5)
    count_dev = TOKENS // TOK_DEV
    rows_dev = TOK_DEV // 4
    mean = rows_dev // count_dev
    index = jnp.arange(count_dev, dtype=jnp.int32)
    levels = jnp.where(index < count_dev // 4, 0, jnp.where(index < 3 * count_dev // 4, mean, 2 * mean)).astype(jnp.int32)
    pattern = jax.random.permutation(keys[0], levels)
    source_perm = jax.random.permutation(keys[1], count_dev)
    target_perm = jax.random.permutation(keys[2], count_dev)
    counts = pattern[(target_perm[None, :] - source_perm[:, None]) % count_dev].astype(jnp.int32)
    running = jnp.cumsum(counts, axis=1).astype(jnp.int32)
    position = jnp.arange(rows_dev, dtype=jnp.int32)
    dest_sorted = jnp.sum((running[:, None, :] <= position[None, :, None]).astype(jnp.int32), axis=2).astype(jnp.int32)
    start = jnp.take_along_axis(running - counts, dest_sorted, axis=1)
    offsets = (jnp.cumsum(counts, axis=0) - counts).astype(jnp.int32)
    pre_slot = jnp.take_along_axis(offsets, dest_sorted, axis=1) + position[None, :] - start
    slot_perms = jax.vmap(lambda kk: jax.random.permutation(kk, rows_dev))(jax.random.split(keys[3], count_dev)).astype(jnp.int32)
    slot_sorted = slot_perms[dest_sorted, pre_slot]
    order = jax.vmap(lambda kk: jax.random.permutation(kk, rows_dev))(jax.random.split(keys[4], count_dev)).astype(jnp.int32)
    dest = jnp.take_along_axis(dest_sorted, order, axis=1)
    slot = jnp.take_along_axis(slot_sorted, order, axis=1)
    return (dest.reshape(MERGED).astype(jnp.int32), slot.reshape(MERGED).astype(jnp.int32))


def draw_dest_device(key, part):
    return routing_tables(key)[0]


def draw_dest_slot(key, part):
    return routing_tables(key)[1]


def shard_levels(own_key, dims, pieces, low, top_value):
    def one(dim, blocks):
        steps = jax.random.uniform(jax.random.fold_in(jax.random.fold_in(own_key, 6), dim), (blocks,), jnp.float32, low / len(pieces), top_value / len(pieces))
        return jnp.repeat(jnp.exp(steps), dims[dim] // blocks).reshape((-1,) + (1,) * (len(dims) - dim - 1))

    level = one(*pieces[0])
    for cut in pieces[1:]:
        level = level * one(*cut)
    return level


def scatter_about(stream_key, extent, scale, limit, pieces=(), held_as=jnp.bfloat16):
    factor_of = shard_levels(stream_key, extent, pieces, -0.22, 0.18) if pieces else 1.0
    drawn = jax.random.normal(stream_key, extent, jnp.float32) * scale * factor_of
    return jnp.minimum(jnp.maximum(drawn, -limit), limit).astype(held_as)


def setup_inputs(seed: int = 0) -> dict:
    arg_keys = jax.random.split(jax.random.key(seed), 15)
    patch_states = draw_patch_states(jax.random.fold_in(arg_keys[14], 71), 0)
    segment_ids = draw_segment_ids(jax.random.fold_in(arg_keys[14], 71), 0)
    first_gain = jnp.clip(1.0 + 0.18 * jax.random.normal(arg_keys[2], (D,), jnp.float32), 0.1, 1.9)
    first_shift = scatter_about(arg_keys[3], (D,), 0.5, 3.0, (), jnp.float32)
    qkv_weight = draw_qkv_weight(jax.random.fold_in(arg_keys[14], 71), 0)
    qkv_bias = scatter_about(arg_keys[5], (3 * D,), 0.5, 3.0, (), jnp.float32)
    out_weight = scatter_about(arg_keys[6], (D, D), D ** -0.5, 0.15625, ((0, 128),))
    out_bias = scatter_about(arg_keys[7], (D,), 0.5, 3.0, (), jnp.float32)
    second_gain = jnp.clip(1.0 + 0.18 * jax.random.normal(arg_keys[8], (D,), jnp.float32), 0.1, 1.9)
    second_shift = scatter_about(arg_keys[9], (D,), 0.5, 3.0, (), jnp.float32)
    merge_weight = scatter_about(arg_keys[10], (D, 4 * D), (4 * D) ** -0.5, 0.078125, ((0, 128),))
    merge_bias = scatter_about(arg_keys[11], (D,), 0.5, 3.0, (), jnp.float32)
    dest_device = draw_dest_device(jax.random.fold_in(arg_keys[14], 71), 0)
    dest_slot = draw_dest_slot(jax.random.fold_in(arg_keys[14], 71), 0)
    return {"patch_states": patch_states, "segment_ids": segment_ids, "first_gain": first_gain, "first_shift": first_shift, "qkv_weight": qkv_weight, "qkv_bias": qkv_bias, "out_weight": out_weight, "out_bias": out_bias, "second_gain": second_gain, "second_shift": second_shift, "merge_weight": merge_weight, "merge_bias": merge_bias, "dest_device": dest_device, "dest_slot": dest_slot}


EPSILON = 1e-06

def layer_norm(states, gain, shift):
    values = states.astype(jnp.float32)
    center = lax.optimization_barrier(jnp.mean(values, axis=-1, keepdims=True))
    spread = lax.optimization_barrier(jnp.mean(jnp.square(values - center), axis=-1, keepdims=True))
    return (values - center) * lax.rsqrt(spread + EPSILON) * gain + shift

def reference(patch_states, segment_ids, first_gain, first_shift, qkv_weight, qkv_bias, out_weight, out_bias, second_gain, second_shift, merge_weight, merge_bias, dest_device, dest_slot):
    packed = TOKENS // TOK_DEV
    states = patch_states.reshape(packed, TOK_DEV, D)
    row_ids = segment_ids.reshape(packed, TOK_DEV)
    scale = 1.0 / HD ** 0.5

    def one_row(pair):
        block, ids_row = pair
        normed = layer_norm(block, first_gain, first_shift).astype(jnp.bfloat16)
        joined = (jnp.dot(normed, qkv_weight.T, preferred_element_type=jnp.float32) + qkv_bias).astype(jnp.bfloat16)
        queries = joined[:, :D].astype(jnp.float32).reshape(TOK_DEV, H, HD)
        keys_all = joined[:, D:2 * D].astype(jnp.float32).reshape(TOK_DEV, H, HD)
        values_all = joined[:, 2 * D:].astype(jnp.float32).reshape(TOK_DEV, H, HD)
        scores = jnp.einsum('qhd,khd->hqk', queries, keys_all, precision=lax.Precision.HIGHEST) * scale
        same = ids_row[:, None] == ids_row[None, :]
        scores = jnp.where(same[None], scores, -jnp.inf)
        top = lax.optimization_barrier(jnp.max(scores, axis=-1, keepdims=True))
        expo = jnp.exp(scores - top)
        probs = (expo / lax.optimization_barrier(jnp.sum(expo, axis=-1, keepdims=True))).astype(jnp.bfloat16)
        attended = jnp.einsum('hqk,khd->qhd', probs.astype(jnp.float32), values_all, precision=lax.Precision.HIGHEST)
        attended = attended.reshape(TOK_DEV, D).astype(jnp.bfloat16)
        hidden = (block.astype(jnp.float32) + jnp.dot(attended, out_weight.T, preferred_element_type=jnp.float32) + out_bias).astype(jnp.bfloat16)
        merged = layer_norm(hidden, second_gain, second_shift).astype(jnp.bfloat16).reshape(TOK_DEV // 4, 4 * D)
        return (jnp.dot(merged, merge_weight.T, preferred_element_type=jnp.float32) + merge_bias).astype(jnp.bfloat16)
    projected = lax.map(one_row, (states, row_ids)).reshape(MERGED, D)
    target = dest_device * MROWS + dest_slot
    return jnp.zeros((MERGED, D), jnp.bfloat16).at[target].set(projected)
```

```python
import functools
import math

import jax
import jax.numpy as jnp
from jax import lax
from jax.experimental import pallas as pl
from jax.experimental.pallas import tpu as pltpu
from jax.sharding import PartitionSpec as P

D = 1280
H = 16
HD = 80


EPSILON = 1e-06


def layer_norm(states, gain, shift):
    values = states.astype(jnp.float32)
    center = jnp.mean(values, axis=-1, keepdims=True)
    spread = jnp.mean(jnp.square(values - center), axis=-1, keepdims=True)
    return (values - center) * lax.rsqrt(spread + EPSILON) * gain + shift


def times_rows(left, piece):
    return lax.dot_general(
        left, piece, (((1,), (1,)), ((), ())), preferred_element_type=jnp.float32
    )


def attention_kernel(scale, q_ref, k_ref, v_ref, qid_ref, kid_ref, o_ref):
    q = q_ref[...]
    k = k_ref[...]
    v = v_ref[...]
    scores = lax.dot_general(
        q, k, (((0,), (0,)), ((), ())), preferred_element_type=jnp.float32
    )
    scores = scores * scale
    same = qid_ref[...] == kid_ref[...]
    masked = jnp.where(same, scores, -jnp.inf)
    top = jnp.max(masked, axis=-1, keepdims=True)
    expo = jnp.exp(masked - top)
    total = jnp.sum(expo, axis=-1, keepdims=True)
    probs = (expo / total).astype(jnp.bfloat16)
    out = lax.dot_general(
        v, probs, (((1,), (1,)), ((), ())), preferred_element_type=jnp.float32
    )
    o_ref[...] = out.astype(o_ref.dtype)


def attention(joined_t, segment_ids, block_q):
    tokens = joined_t.shape[1]
    scale = 1.0 / math.sqrt(HD)
    qid = segment_ids.reshape(tokens, 1)
    kid = segment_ids.reshape(1, tokens)
    flops = 4 * H * tokens * tokens * HD
    cost = pl.CostEstimate(
        flops=flops,
        transcendentals=H * tokens * tokens,
        bytes_accessed=joined_t.size * 2 + tokens * D * 2,
    )
    return pl.pallas_call(
        functools.partial(attention_kernel, scale),
        out_shape=jax.ShapeDtypeStruct((D, tokens), jnp.bfloat16),
        grid=(H, tokens // block_q),
        in_specs=[
            pl.BlockSpec((HD, block_q), lambda h, i: (h, i)),
            pl.BlockSpec((HD, tokens), lambda h, i: (H + h, 0)),
            pl.BlockSpec((HD, tokens), lambda h, i: (2 * H + h, 0)),
            pl.BlockSpec((block_q, 1), lambda h, i: (i, 0)),
            pl.BlockSpec((1, tokens), lambda h, i: (0, 0)),
        ],
        out_specs=pl.BlockSpec((HD, block_q), lambda h, i: (h, i)),
        cost_estimate=cost,
    )(joined_t, joined_t, joined_t, qid, kid)


def per_device(
    patch_states,
    segment_ids,
    first_gain,
    first_shift,
    qkv_weight,
    qkv_bias,
    out_weight,
    out_bias,
    second_gain,
    second_shift,
    merge_weight,
    merge_bias,
    dest_device,
    dest_slot,
):
    tokens = patch_states.shape[0]
    width = D
    axes = ("fsdp", "dp")

    qkv_full = lax.all_gather(qkv_weight, axes, axis=0, tiled=True)
    out_rows = out_weight.shape[0]
    merge_rows = merge_weight.shape[0]
    lanes = 128
    flat = jnp.concatenate(
        [out_weight.reshape(-1, lanes), merge_weight.reshape(-1, lanes)], axis=0
    )[None]
    qkv_full, flat = lax.optimization_barrier((qkv_full, flat))
    rest = lax.all_gather(flat, axes, axis=0, tiled=True)
    devices = rest.shape[0]
    out_cut = out_rows * width // lanes
    out_full = rest[:, :out_cut].reshape(devices * out_rows, width)
    merge_full = rest[:, out_cut:].reshape(devices * merge_rows, 4 * width)

    normed = layer_norm(patch_states, first_gain, first_shift).astype(jnp.bfloat16)
    joined_t = lax.dot_general(
        qkv_full, normed, (((1,), (1,)), ((), ())), preferred_element_type=jnp.float32
    )
    joined_t = (joined_t + qkv_bias[:, None]).astype(jnp.bfloat16)

    attended_t = attention(joined_t, segment_ids, 512)

    projected_att = lax.dot_general(
        attended_t, out_full, (((0,), (1,)), ((), ())), preferred_element_type=jnp.float32
    )
    hidden = (patch_states.astype(jnp.float32) + projected_att + out_bias).astype(
        jnp.bfloat16
    )
    merged = (
        layer_norm(hidden, second_gain, second_shift)
        .astype(jnp.bfloat16)
        .reshape(tokens // 4, 4 * width)
    )
    projected = (times_rows(merged, merge_full) + merge_bias).astype(jnp.bfloat16)

    fsdp_count = lax.axis_size("fsdp")
    dp_count = lax.axis_size("dp")
    count_dev = fsdp_count * dp_count
    row_count = tokens // 4
    capacity = 2 * (row_count // count_dev)
    matches = (dest_device[:, None] == jnp.arange(count_dev, dtype=jnp.int32)[None, :]).astype(
        jnp.int32
    )
    earlier = jnp.cumsum(matches, axis=0) - matches
    rank = jnp.sum(earlier * matches, axis=1)
    position = dest_device * capacity + rank
    rows_out = jnp.zeros((count_dev * capacity, width), jnp.bfloat16).at[position].set(projected)
    slots_out = jnp.full((count_dev * capacity,), row_count, jnp.int32).at[position].set(dest_slot)
    got_rows, got_slots = (
        lax.all_to_all(
            rows_out.reshape(count_dev, capacity, width),
            axes,
            split_axis=0,
            concat_axis=0,
            tiled=True,
        ),
        lax.all_to_all(
            slots_out.reshape(count_dev, capacity),
            axes,
            split_axis=0,
            concat_axis=0,
            tiled=True,
        ),
    )
    requests = (
        jnp.zeros((row_count, width), jnp.bfloat16)
        .at[got_slots.reshape(-1)]
        .set(got_rows.reshape(-1, width), mode="drop")
    )
    return requests


def solution(mesh):
    in_specs = (
        P(("fsdp", "dp"), None),
        P(("fsdp", "dp")),
        P(),
        P(),
        P(("fsdp", "dp"), None),
        P(),
        P(("fsdp", "dp"), None),
        P(),
        P(),
        P(),
        P(("fsdp", "dp"), None),
        P(),
        P(("fsdp", "dp")),
        P(("fsdp", "dp")),
    )
    out_specs = P(("fsdp", "dp"), None)
    return jax.shard_map(
        per_device, mesh=mesh, in_specs=in_specs, out_specs=out_specs, check_vma=False
    )
```

```python
import functools
import math

import jax
import jax.numpy as jnp
from jax import lax
from jax.experimental import pallas as pl
from jax.experimental.pallas import tpu as pltpu
from jax.sharding import PartitionSpec as P

D = 1280
H = 16
HD = 80


EPSILON = 1e-06


def layer_norm(states, gain, shift):
    values = states.astype(jnp.float32)
    center = jnp.mean(values, axis=-1, keepdims=True)
    spread = jnp.mean(jnp.square(values - center), axis=-1, keepdims=True)
    return (values - center) * lax.rsqrt(spread + EPSILON) * gain + shift


def times_rows(left, piece):
    return lax.dot_general(
        left, piece, (((1,), (1,)), ((), ())), preferred_element_type=jnp.float32
    )


def attention_kernel(scale, q_ref, k_ref, v_ref, qid_ref, kid_ref, o_ref):
    q = q_ref[...]
    k = k_ref[...]
    v = v_ref[...]
    scores = lax.dot_general(
        q, k, (((0,), (0,)), ((), ())), preferred_element_type=jnp.float32
    )
    scores = scores * scale
    same = qid_ref[...] == kid_ref[...]
    masked = jnp.where(same, scores, -jnp.inf)
    top = jnp.max(masked, axis=-1, keepdims=True)
    expo = jnp.exp(masked - top)
    total = jnp.sum(expo, axis=-1, keepdims=True)
    probs = (expo * (1.0 / total)).astype(jnp.bfloat16)
    out = lax.dot_general(
        v, probs, (((1,), (1,)), ((), ())), preferred_element_type=jnp.float32
    )
    o_ref[...] = out.astype(o_ref.dtype)


def attention(joined_t, segment_ids, block_q):
    tokens = joined_t.shape[1]
    scale = 1.0 / math.sqrt(HD)
    qid = segment_ids.reshape(tokens, 1)
    kid = segment_ids.reshape(1, tokens)
    flops = 4 * H * tokens * tokens * HD
    cost = pl.CostEstimate(
        flops=flops,
        transcendentals=H * tokens * tokens,
        bytes_accessed=joined_t.size * 2 + tokens * D * 2,
    )
    return pl.pallas_call(
        functools.partial(attention_kernel, scale),
        out_shape=jax.ShapeDtypeStruct((D, tokens), jnp.bfloat16),
        grid=(H, tokens // block_q),
        in_specs=[
            pl.BlockSpec((HD, block_q), lambda h, i: (h, i)),
            pl.BlockSpec((HD, tokens), lambda h, i: (H + h, 0)),
            pl.BlockSpec((HD, tokens), lambda h, i: (2 * H + h, 0)),
            pl.BlockSpec((block_q, 1), lambda h, i: (i, 0)),
            pl.BlockSpec((1, tokens), lambda h, i: (0, 0)),
        ],
        out_specs=pl.BlockSpec((HD, block_q), lambda h, i: (h, i)),
        cost_estimate=cost,
    )(joined_t, joined_t, joined_t, qid, kid)


def per_device(
    patch_states,
    segment_ids,
    first_gain,
    first_shift,
    qkv_weight,
    qkv_bias,
    out_weight,
    out_bias,
    second_gain,
    second_shift,
    merge_weight,
    merge_bias,
    dest_device,
    dest_slot,
):
    tokens = patch_states.shape[0]
    width = D
    axes = ("fsdp", "dp")

    qkv_rows = qkv_weight.shape[0]
    out_rows = out_weight.shape[0]
    merge_rows = merge_weight.shape[0]
    tile_rows = 16
    first_parts = lax.all_gather(
        jnp.concatenate([qkv_weight, out_weight], axis=0), axes, axis=0, tiled=False
    )
    merge_padded = jnp.concatenate(
        [merge_weight, jnp.zeros((tile_rows - merge_rows, 4 * width), merge_weight.dtype)],
        axis=0,
    )
    first_parts, merge_padded = lax.optimization_barrier((first_parts, merge_padded))
    merge_parts = lax.all_gather(merge_padded, axes, axis=0, tiled=False)
    devices = first_parts.shape[0]
    qkv_full = first_parts[:, :qkv_rows].reshape(devices * qkv_rows, width)
    out_full = first_parts[:, qkv_rows:].reshape(devices * out_rows, width)
    merge_full = merge_parts.reshape(devices * tile_rows, 4 * width)

    normed = layer_norm(patch_states, first_gain, first_shift).astype(jnp.bfloat16)
    joined_t = lax.dot_general(
        qkv_full, normed, (((1,), (1,)), ((), ())), preferred_element_type=jnp.float32
    )
    joined_t = (joined_t + qkv_bias[:, None]).astype(jnp.bfloat16)

    attended_t = attention(joined_t, segment_ids, 512)

    projected_att = lax.dot_general(
        attended_t, out_full, (((0,), (1,)), ((), ())), preferred_element_type=jnp.float32
    )
    hidden = (patch_states.astype(jnp.float32) + projected_att + out_bias).astype(
        jnp.bfloat16
    )
    merged = (
        layer_norm(hidden, second_gain, second_shift)
        .astype(jnp.bfloat16)
        .reshape(tokens // 4, 4 * width)
    )
    projected_padded = times_rows(merged, merge_full).reshape(
        tokens // 4, devices, tile_rows
    )
    projected = projected_padded[:, :, :merge_rows].reshape(tokens // 4, width)
    projected = (projected + merge_bias).astype(jnp.bfloat16)

    fsdp_count = lax.axis_size("fsdp")
    dp_count = lax.axis_size("dp")
    count_dev = fsdp_count * dp_count
    row_count = tokens // 4
    capacity = 2 * (row_count // count_dev)
    matches = (dest_device[:, None] == jnp.arange(count_dev, dtype=jnp.int32)[None, :]).astype(
        jnp.int32
    )
    earlier = jnp.cumsum(matches, axis=0) - matches
    rank = jnp.sum(earlier * matches, axis=1)
    position = dest_device * capacity + rank
    rows_out = jnp.zeros((count_dev * capacity, width), jnp.bfloat16).at[position].set(projected)
    slots_out = jnp.full((count_dev * capacity,), row_count, jnp.int32).at[position].set(dest_slot)
    got_rows, got_slots = (
        lax.all_to_all(
            rows_out.reshape(count_dev, capacity, width),
            axes,
            split_axis=0,
            concat_axis=0,
            tiled=True,
        ),
        lax.all_to_all(
            slots_out.reshape(count_dev, capacity),
            axes,
            split_axis=0,
            concat_axis=0,
            tiled=True,
        ),
    )
    requests = (
        jnp.zeros((row_count, width), jnp.bfloat16)
        .at[got_slots.reshape(-1)]
        .set(got_rows.reshape(-1, width), mode="drop")
    )
    return requests


def solution(mesh):
    in_specs = (
        P(("fsdp", "dp"), None),
        P(("fsdp", "dp")),
        P(),
        P(),
        P(("fsdp", "dp"), None),
        P(),
        P(("fsdp", "dp"), None),
        P(),
        P(),
        P(),
        P(("fsdp", "dp"), None),
        P(),
        P(("fsdp", "dp")),
        P(("fsdp", "dp")),
    )
    out_specs = P(("fsdp", "dp"), None)
    return jax.shard_map(
        per_device, mesh=mesh, in_specs=in_specs, out_specs=out_specs, check_vma=False
    )
```

```python
import functools
import math

import jax
import jax.numpy as jnp
from jax import lax
from jax.experimental import pallas as pl
from jax.experimental.pallas import tpu as pltpu
from jax.sharding import PartitionSpec as P

D = 1280
H = 16
HD = 80


EPSILON = 1e-06


def layer_norm(states, gain, shift):
    values = states.astype(jnp.float32)
    center = jnp.mean(values, axis=-1, keepdims=True)
    spread = jnp.mean(jnp.square(values - center), axis=-1, keepdims=True)
    return (values - center) * lax.rsqrt(spread + EPSILON) * gain + shift


def times_rows(left, piece):
    return lax.dot_general(
        left, piece, (((1,), (1,)), ((), ())), preferred_element_type=jnp.float32
    )


def attention_kernel(scale, q_ref, k_ref, v_ref, qid_ref, kid_ref, o_ref):
    q = q_ref[...]
    k = k_ref[...]
    v = v_ref[...]
    scores = lax.dot_general(
        q, k, (((0,), (0,)), ((), ())), preferred_element_type=jnp.float32
    )
    scores = scores * scale
    same = qid_ref[...] == kid_ref[...]
    masked = jnp.where(same, scores, -jnp.inf)
    top = jnp.max(masked, axis=-1, keepdims=True)
    expo = jnp.exp(masked - top)
    total = jnp.sum(expo, axis=-1, keepdims=True)
    probs = (expo / total).astype(jnp.bfloat16)
    out = lax.dot_general(
        v, probs, (((1,), (1,)), ((), ())), preferred_element_type=jnp.float32
    )
    o_ref[...] = out.astype(o_ref.dtype)


def attention(joined_t, segment_ids, block_q):
    tokens = joined_t.shape[1]
    scale = 1.0 / math.sqrt(HD)
    qid = segment_ids.reshape(tokens, 1)
    kid = segment_ids.reshape(1, tokens)
    flops = 4 * H * tokens * tokens * HD
    cost = pl.CostEstimate(
        flops=flops,
        transcendentals=H * tokens * tokens,
        bytes_accessed=joined_t.size * 2 + tokens * D * 2,
    )
    return pl.pallas_call(
        functools.partial(attention_kernel, scale),
        out_shape=jax.ShapeDtypeStruct((D, tokens), jnp.bfloat16),
        grid=(H, tokens // block_q),
        in_specs=[
            pl.BlockSpec((HD, block_q), lambda h, i: (h, i)),
            pl.BlockSpec((HD, tokens), lambda h, i: (H + h, 0)),
            pl.BlockSpec((HD, tokens), lambda h, i: (2 * H + h, 0)),
            pl.BlockSpec((block_q, 1), lambda h, i: (i, 0)),
            pl.BlockSpec((1, tokens), lambda h, i: (0, 0)),
        ],
        out_specs=pl.BlockSpec((HD, block_q), lambda h, i: (h, i)),
        cost_estimate=cost,
    )(joined_t, joined_t, joined_t, qid, kid)


def per_device(
    patch_states,
    segment_ids,
    first_gain,
    first_shift,
    qkv_weight,
    qkv_bias,
    out_weight,
    out_bias,
    second_gain,
    second_shift,
    merge_weight,
    merge_bias,
    dest_device,
    dest_slot,
):
    tokens = patch_states.shape[0]
    width = D
    axes = ("fsdp", "dp")

    qkv_full = lax.all_gather(qkv_weight, axes, axis=0, tiled=False)
    out_rows = out_weight.shape[0]
    merge_rows = merge_weight.shape[0]
    tile_rows = 16
    wide = 4 * width
    out_pad_rows = -(-out_rows * width // wide) * (wide // width)
    out_packed = jnp.concatenate(
        [out_weight, jnp.zeros((out_pad_rows - out_rows, width), out_weight.dtype)], axis=0
    ).reshape(-1, wide)
    packed_rows = out_packed.shape[0]
    second = jnp.concatenate(
        [
            merge_weight,
            out_packed,
            jnp.zeros((tile_rows - merge_rows - packed_rows, wide), merge_weight.dtype),
        ],
        axis=0,
    )
    qkv_full, second = lax.optimization_barrier((qkv_full, second))
    second_parts = lax.all_gather(second, axes, axis=0, tiled=False)
    devices = second_parts.shape[0]
    qkv_full = qkv_full.reshape(devices * qkv_weight.shape[0], width)
    out_full = (
        second_parts[:, merge_rows : merge_rows + packed_rows]
        .reshape(devices, out_pad_rows, width)[:, :out_rows]
        .reshape(devices * out_rows, width)
    )
    merge_full = second_parts.reshape(devices * tile_rows, wide)

    normed = layer_norm(patch_states, first_gain, first_shift).astype(jnp.bfloat16)
    joined_t = lax.dot_general(
        qkv_full, normed, (((1,), (1,)), ((), ())), preferred_element_type=jnp.float32
    )
    joined_t = (joined_t + qkv_bias[:, None]).astype(jnp.bfloat16)

    attended_t = attention(joined_t, segment_ids, 512)

    projected_att = lax.dot_general(
        attended_t, out_full, (((0,), (1,)), ((), ())), preferred_element_type=jnp.float32
    )
    hidden = (patch_states.astype(jnp.float32) + projected_att + out_bias).astype(
        jnp.bfloat16
    )
    merged = (
        layer_norm(hidden, second_gain, second_shift)
        .astype(jnp.bfloat16)
        .reshape(tokens // 4, 4 * width)
    )
    projected_padded = lax.optimization_barrier(times_rows(merged, merge_full))
    projected = projected_padded.reshape(tokens // 4, devices, tile_rows)[:, :, :merge_rows]
    projected = (projected.reshape(tokens // 4, width) + merge_bias).astype(jnp.bfloat16)

    fsdp_count = lax.axis_size("fsdp")
    dp_count = lax.axis_size("dp")
    count_dev = fsdp_count * dp_count
    row_count = tokens // 4
    capacity = 2 * (row_count // count_dev)
    matches = (dest_device[:, None] == jnp.arange(count_dev, dtype=jnp.int32)[None, :]).astype(
        jnp.int32
    )
    earlier = jnp.cumsum(matches, axis=0) - matches
    rank = jnp.sum(earlier * matches, axis=1)
    position = dest_device * capacity + rank
    rows_out = jnp.zeros((count_dev * capacity, width), jnp.bfloat16).at[position].set(projected)
    slots_out = jnp.full((count_dev * capacity,), row_count, jnp.int32).at[position].set(dest_slot)
    got_rows, got_slots = (
        lax.all_to_all(
            rows_out.reshape(count_dev, capacity, width),
            axes,
            split_axis=0,
            concat_axis=0,
            tiled=True,
        ),
        lax.all_to_all(
            slots_out.reshape(count_dev, capacity),
            axes,
            split_axis=0,
            concat_axis=0,
            tiled=True,
        ),
    )
    requests = (
        jnp.zeros((row_count, width), jnp.bfloat16)
        .at[got_slots.reshape(-1)]
        .set(got_rows.reshape(-1, width), mode="drop")
    )
    return requests


def solution(mesh):
    in_specs = (
        P(("fsdp", "dp"), None),
        P(("fsdp", "dp")),
        P(),
        P(),
        P(("fsdp", "dp"), None),
        P(),
        P(("fsdp", "dp"), None),
        P(),
        P(),
        P(),
        P(("fsdp", "dp"), None),
        P(),
        P(("fsdp", "dp")),
        P(("fsdp", "dp")),
    )
    out_specs = P(("fsdp", "dp"), None)
    return jax.shard_map(
        per_device, mesh=mesh, in_specs=in_specs, out_specs=out_specs, check_vma=False
    )
```

```python
import functools
import math

import jax
import jax.numpy as jnp
from jax import lax
from jax.experimental import pallas as pl
from jax.experimental.pallas import tpu as pltpu
from jax.sharding import PartitionSpec as P

D = 1280
H = 16
HD = 80


EPSILON = 1e-06


def layer_norm(states, gain, shift):
    values = states.astype(jnp.float32)
    center = jnp.mean(values, axis=-1, keepdims=True)
    spread = jnp.mean(jnp.square(values - center), axis=-1, keepdims=True)
    return (values - center) * lax.rsqrt(spread + EPSILON) * gain + shift


def times_rows(left, piece):
    return lax.dot_general(
        left, piece, (((1,), (1,)), ((), ())), preferred_element_type=jnp.float32
    )


def attention_kernel(scale, q_ref, k_ref, v_ref, qid_ref, kid_ref, o_ref):
    q = q_ref[...]
    k = k_ref[...]
    v = v_ref[...]
    scores = lax.dot_general(
        q, k, (((0,), (0,)), ((), ())), preferred_element_type=jnp.float32
    )
    scores = scores * scale
    same = qid_ref[...] == kid_ref[...]
    masked = jnp.where(same, scores, -jnp.inf)
    top = jnp.max(masked, axis=-1, keepdims=True)
    expo = jnp.exp(masked - top)
    total = jnp.sum(expo, axis=-1, keepdims=True)
    probs = (expo / total).astype(jnp.bfloat16)
    out = lax.dot_general(
        v, probs, (((1,), (1,)), ((), ())), preferred_element_type=jnp.float32
    )
    o_ref[...] = out.astype(o_ref.dtype)


def attention(joined_t, segment_ids, block_q):
    tokens = joined_t.shape[1]
    scale = 1.0 / math.sqrt(HD)
    qid = segment_ids.reshape(tokens, 1)
    kid = segment_ids.reshape(1, tokens)
    flops = 4 * H * tokens * tokens * HD
    cost = pl.CostEstimate(
        flops=flops,
        transcendentals=H * tokens * tokens,
        bytes_accessed=joined_t.size * 2 + tokens * D * 2,
    )
    return pl.pallas_call(
        functools.partial(attention_kernel, scale),
        out_shape=jax.ShapeDtypeStruct((D, tokens), jnp.bfloat16),
        grid=(H, tokens // block_q),
        in_specs=[
            pl.BlockSpec((HD, block_q), lambda h, i: (h, i)),
            pl.BlockSpec((HD, tokens), lambda h, i: (H + h, 0)),
            pl.BlockSpec((HD, tokens), lambda h, i: (2 * H + h, 0)),
            pl.BlockSpec((block_q, 1), lambda h, i: (i, 0)),
            pl.BlockSpec((1, tokens), lambda h, i: (0, 0)),
        ],
        out_specs=pl.BlockSpec((HD, block_q), lambda h, i: (h, i)),
        cost_estimate=cost,
    )(joined_t, joined_t, joined_t, qid, kid)


def per_device(
    patch_states,
    segment_ids,
    first_gain,
    first_shift,
    qkv_weight,
    qkv_bias,
    out_weight,
    out_bias,
    second_gain,
    second_shift,
    merge_weight,
    merge_bias,
    dest_device,
    dest_slot,
):
    tokens = patch_states.shape[0]
    width = D
    axes = ("fsdp", "dp")

    qkv_full = lax.all_gather(qkv_weight, axes, axis=0, tiled=False)
    out_rows = out_weight.shape[0]
    merge_rows = merge_weight.shape[0]
    tile_rows = 16
    wide = 4 * width
    second = jnp.concatenate([merge_weight, out_weight], axis=1)
    second = jnp.concatenate(
        [second, jnp.zeros((tile_rows - merge_rows, wide + width), second.dtype)], axis=0
    )
    qkv_full, second = lax.optimization_barrier((qkv_full, second))
    second_parts = lax.all_gather(second, axes, axis=0, tiled=False)
    devices = second_parts.shape[0]
    qkv_full = qkv_full.reshape(devices * qkv_weight.shape[0], width)
    second_full = second_parts.reshape(devices * tile_rows, wide + width)
    out_padded = second_full[:, wide:]

    normed = layer_norm(patch_states, first_gain, first_shift).astype(jnp.bfloat16)
    joined_t = lax.dot_general(
        qkv_full, normed, (((1,), (1,)), ((), ())), preferred_element_type=jnp.float32
    )
    joined_t = (joined_t + qkv_bias[:, None]).astype(jnp.bfloat16)

    attended_t = attention(joined_t, segment_ids, 512)

    projected_att = lax.optimization_barrier(
        lax.dot_general(
            attended_t, out_padded, (((0,), (1,)), ((), ())), preferred_element_type=jnp.float32
        )
    )
    projected_att = projected_att.reshape(tokens, devices, tile_rows)[:, :, :out_rows]
    hidden = (
        patch_states.astype(jnp.float32) + projected_att.reshape(tokens, width) + out_bias
    ).astype(jnp.bfloat16)
    merged = (
        layer_norm(hidden, second_gain, second_shift)
        .astype(jnp.bfloat16)
        .reshape(tokens // 4, 4 * width)
    )
    merged_wide = jnp.concatenate([merged, jnp.zeros((tokens // 4, width), merged.dtype)], axis=1)
    projected_padded = lax.optimization_barrier(times_rows(merged_wide, second_full))
    projected = projected_padded.reshape(tokens // 4, devices, tile_rows)[:, :, :merge_rows]
    projected = (projected.reshape(tokens // 4, width) + merge_bias).astype(jnp.bfloat16)

    fsdp_count = lax.axis_size("fsdp")
    dp_count = lax.axis_size("dp")
    count_dev = fsdp_count * dp_count
    row_count = tokens // 4
    capacity = 2 * (row_count // count_dev)
    matches = (dest_device[:, None] == jnp.arange(count_dev, dtype=jnp.int32)[None, :]).astype(
        jnp.int32
    )
    earlier = jnp.cumsum(matches, axis=0) - matches
    rank = jnp.sum(earlier * matches, axis=1)
    position = dest_device * capacity + rank
    lanes = 128
    slot_block = jnp.broadcast_to(dest_slot.astype(jnp.bfloat16)[:, None], (row_count, lanes))
    payload = jnp.concatenate([projected, slot_block], axis=1)
    place = (
        position[None, :] == jnp.arange(count_dev * capacity, dtype=jnp.int32)[:, None]
    ).astype(jnp.bfloat16)
    rows_out = jnp.dot(place, payload, preferred_element_type=jnp.float32)
    empty = (jnp.sum(place, axis=1, keepdims=True) == 0)
    slot_lane = jnp.where(empty, float(row_count), rows_out[:, width:])
    rows_out = jnp.concatenate([rows_out[:, :width], slot_lane], axis=1).astype(jnp.bfloat16)
    got = lax.all_to_all(
        rows_out.reshape(count_dev, capacity, width + lanes),
        axes,
        split_axis=0,
        concat_axis=0,
        tiled=True,
    ).reshape(count_dev * capacity, width + lanes)
    got_slots = got[:, width].astype(jnp.int32)
    pick = (
        got_slots[None, :] == jnp.arange(row_count, dtype=jnp.int32)[:, None]
    ).astype(jnp.bfloat16)
    requests = jnp.dot(pick, got[:, :width], preferred_element_type=jnp.float32).astype(
        jnp.bfloat16
    )
    return requests


def solution(mesh):
    in_specs = (
        P(("fsdp", "dp"), None),
        P(("fsdp", "dp")),
        P(),
        P(),
        P(("fsdp", "dp"), None),
        P(),
        P(("fsdp", "dp"), None),
        P(),
        P(),
        P(),
        P(("fsdp", "dp"), None),
        P(),
        P(("fsdp", "dp")),
        P(("fsdp", "dp")),
    )
    out_specs = P(("fsdp", "dp"), None)
    return jax.shard_map(
        per_device, mesh=mesh, in_specs=in_specs, out_specs=out_specs, check_vma=False
    )
```

```python
import functools
import math

import jax
import jax.numpy as jnp
from jax import lax
from jax.experimental import pallas as pl
from jax.experimental.pallas import tpu as pltpu
from jax.sharding import PartitionSpec as P

D = 1280
H = 16
HD = 80


EPSILON = 1e-06


def layer_norm(states, gain, shift):
    values = states.astype(jnp.float32)
    center = jnp.mean(values, axis=-1, keepdims=True)
    spread = jnp.mean(jnp.square(values - center), axis=-1, keepdims=True)
    return (values - center) * lax.rsqrt(spread + EPSILON) * gain + shift


def times_rows(left, piece):
    return lax.dot_general(
        left, piece, (((1,), (1,)), ((), ())), preferred_element_type=jnp.float32
    )


def attention_kernel(scale, q_ref, k_ref, v_ref, qid_ref, kid_ref, o_ref):
    q = q_ref[...]
    k = k_ref[...]
    v = v_ref[...]
    scores = lax.dot_general(
        q, k, (((0,), (0,)), ((), ())), preferred_element_type=jnp.float32
    )
    scores = scores * scale
    same = qid_ref[...] == kid_ref[...]
    masked = jnp.where(same, scores, -jnp.inf)
    top = jnp.max(masked, axis=-1, keepdims=True)
    expo = jnp.exp(masked - top)
    total = jnp.sum(expo, axis=-1, keepdims=True)
    probs = (expo / total).astype(jnp.bfloat16)
    out = lax.dot_general(
        v, probs, (((1,), (1,)), ((), ())), preferred_element_type=jnp.float32
    )
    o_ref[...] = out.astype(o_ref.dtype)


def attention(joined_t, segment_ids, block_q):
    tokens = joined_t.shape[1]
    scale = 1.0 / math.sqrt(HD)
    qid = segment_ids.reshape(tokens, 1)
    kid = segment_ids.reshape(1, tokens)
    flops = 4 * H * tokens * tokens * HD
    cost = pl.CostEstimate(
        flops=flops,
        transcendentals=H * tokens * tokens,
        bytes_accessed=joined_t.size * 2 + tokens * D * 2,
    )
    return pl.pallas_call(
        functools.partial(attention_kernel, scale),
        out_shape=jax.ShapeDtypeStruct((D, tokens), jnp.bfloat16),
        grid=(H, tokens // block_q),
        in_specs=[
            pl.BlockSpec((HD, block_q), lambda h, i: (h, i)),
            pl.BlockSpec((HD, tokens), lambda h, i: (H + h, 0)),
            pl.BlockSpec((HD, tokens), lambda h, i: (2 * H + h, 0)),
            pl.BlockSpec((block_q, 1), lambda h, i: (i, 0)),
            pl.BlockSpec((1, tokens), lambda h, i: (0, 0)),
        ],
        out_specs=pl.BlockSpec((HD, block_q), lambda h, i: (h, i)),
        cost_estimate=cost,
    )(joined_t, joined_t, joined_t, qid, kid)


def per_device(
    patch_states,
    segment_ids,
    first_gain,
    first_shift,
    qkv_weight,
    qkv_bias,
    out_weight,
    out_bias,
    second_gain,
    second_shift,
    merge_weight,
    merge_bias,
    dest_device,
    dest_slot,
):
    tokens = patch_states.shape[0]
    width = D
    axes = ("fsdp", "dp")

    qkv_parts = lax.all_gather(qkv_weight, axes, axis=0, tiled=False)
    out_rows = out_weight.shape[0]
    merge_rows = merge_weight.shape[0]
    lanes = 128
    flat = jnp.concatenate(
        [out_weight.reshape(-1, lanes), merge_weight.reshape(-1, lanes)], axis=0
    )
    qkv_parts, flat = lax.optimization_barrier((qkv_parts, flat))
    rest = lax.all_gather(flat, axes, axis=0, tiled=False)
    devices = rest.shape[0]
    qkv_full = qkv_parts.reshape(devices * qkv_weight.shape[0], width)
    out_cut = out_rows * width // lanes
    out_full = rest[:, :out_cut].reshape(devices * out_rows, width)
    merge_full = rest[:, out_cut:].reshape(devices * merge_rows, 4 * width)

    normed = layer_norm(patch_states, first_gain, first_shift).astype(jnp.bfloat16)
    joined_t = lax.dot_general(
        qkv_full, normed, (((1,), (1,)), ((), ())), preferred_element_type=jnp.float32
    )
    joined_t = (joined_t + qkv_bias[:, None]).astype(jnp.bfloat16)

    attended_t = attention(joined_t, segment_ids, 512)

    projected_att = lax.dot_general(
        attended_t, out_full, (((0,), (1,)), ((), ())), preferred_element_type=jnp.float32
    )
    hidden = (patch_states.astype(jnp.float32) + projected_att + out_bias).astype(
        jnp.bfloat16
    )
    merged = (
        layer_norm(hidden, second_gain, second_shift)
        .astype(jnp.bfloat16)
        .reshape(tokens // 4, 4 * width)
    )
    projected = (times_rows(merged, merge_full) + merge_bias).astype(jnp.bfloat16)

    fsdp_count = lax.axis_size("fsdp")
    dp_count = lax.axis_size("dp")
    count_dev = fsdp_count * dp_count
    row_count = tokens // 4
    capacity = 2 * (row_count // count_dev)
    matches = (dest_device[:, None] == jnp.arange(count_dev, dtype=jnp.int32)[None, :]).astype(
        jnp.int32
    )
    earlier = jnp.cumsum(matches, axis=0) - matches
    rank = jnp.sum(earlier * matches, axis=1)
    position = dest_device * capacity + rank
    lanes = 128
    slot_block = jnp.broadcast_to(dest_slot.astype(jnp.bfloat16)[:, None], (row_count, lanes))
    payload = jnp.concatenate([projected, slot_block], axis=1)
    place = (
        position[None, :] == jnp.arange(count_dev * capacity, dtype=jnp.int32)[:, None]
    ).astype(jnp.bfloat16)
    rows_out = jnp.dot(place, payload, preferred_element_type=jnp.float32)
    empty = (jnp.sum(place, axis=1, keepdims=True) == 0)
    slot_lane = jnp.where(empty, float(row_count), rows_out[:, width:])
    rows_out = jnp.concatenate([rows_out[:, :width], slot_lane], axis=1).astype(jnp.bfloat16)
    got = lax.all_to_all(
        rows_out.reshape(count_dev, capacity, width + lanes),
        axes,
        split_axis=0,
        concat_axis=0,
        tiled=True,
    ).reshape(count_dev * capacity, width + lanes)
    got_slots = got[:, width].astype(jnp.int32)
    pick = (
        got_slots[None, :] == jnp.arange(row_count, dtype=jnp.int32)[:, None]
    ).astype(jnp.bfloat16)
    requests = jnp.dot(pick, got[:, :width], preferred_element_type=jnp.float32).astype(
        jnp.bfloat16
    )
    return requests


def solution(mesh):
    in_specs = (
        P(("fsdp", "dp"), None),
        P(("fsdp", "dp")),
        P(),
        P(),
        P(("fsdp", "dp"), None),
        P(),
        P(("fsdp", "dp"), None),
        P(),
        P(),
        P(),
        P(("fsdp", "dp"), None),
        P(),
        P(("fsdp", "dp")),
        P(("fsdp", "dp")),
    )
    out_specs = P(("fsdp", "dp"), None)
    return jax.shard_map(
        per_device, mesh=mesh, in_specs=in_specs, out_specs=out_specs, check_vma=False
    )
```

```python
import functools
import math

import jax
import jax.numpy as jnp
from jax import lax
from jax.experimental import pallas as pl
from jax.experimental.pallas import tpu as pltpu
from jax.sharding import PartitionSpec as P

D = 1280
H = 16
HD = 80


EPSILON = 1e-06


def layer_norm(states, gain, shift):
    values = states.astype(jnp.float32)
    center = jnp.mean(values, axis=-1, keepdims=True)
    spread = jnp.mean(jnp.square(values - center), axis=-1, keepdims=True)
    return (values - center) * lax.rsqrt(spread + EPSILON) * gain + shift


def times_rows(left, piece):
    return lax.dot_general(
        left, piece, (((1,), (1,)), ((), ())), preferred_element_type=jnp.float32
    )


def attention_kernel(scale, q_ref, k_ref, v_ref, qid_ref, kid_ref, o_ref):
    q = q_ref[...]
    k = k_ref[...]
    v = v_ref[...]
    scores = lax.dot_general(
        q, k, (((0,), (0,)), ((), ())), preferred_element_type=jnp.float32
    )
    scores = scores * scale
    same = qid_ref[...] == kid_ref[...]
    masked = jnp.where(same, scores, -jnp.inf)
    top = jnp.max(masked, axis=-1, keepdims=True)
    expo = jnp.exp(masked - top)
    total = jnp.sum(expo, axis=-1, keepdims=True)
    probs = (expo / total).astype(jnp.bfloat16)
    out = lax.dot_general(
        v, probs, (((1,), (1,)), ((), ())), preferred_element_type=jnp.float32
    )
    o_ref[...] = out.astype(o_ref.dtype)


def attention(joined_t, segment_ids, block_q):
    tokens = joined_t.shape[1]
    scale = 1.0 / math.sqrt(HD)
    qid = segment_ids.reshape(tokens, 1)
    kid = segment_ids.reshape(1, tokens)
    flops = 4 * H * tokens * tokens * HD
    cost = pl.CostEstimate(
        flops=flops,
        transcendentals=H * tokens * tokens,
        bytes_accessed=joined_t.size * 2 + tokens * D * 2,
    )
    return pl.pallas_call(
        functools.partial(attention_kernel, scale),
        out_shape=jax.ShapeDtypeStruct((D, tokens), jnp.bfloat16),
        grid=(H, tokens // block_q),
        in_specs=[
            pl.BlockSpec((HD, block_q), lambda h, i: (h, i)),
            pl.BlockSpec((HD, tokens), lambda h, i: (H + h, 0)),
            pl.BlockSpec((HD, tokens), lambda h, i: (2 * H + h, 0)),
            pl.BlockSpec((block_q, 1), lambda h, i: (i, 0)),
            pl.BlockSpec((1, tokens), lambda h, i: (0, 0)),
        ],
        out_specs=pl.BlockSpec((HD, block_q), lambda h, i: (h, i)),
        cost_estimate=cost,
    )(joined_t, joined_t, joined_t, qid, kid)


def per_device(
    patch_states,
    segment_ids,
    first_gain,
    first_shift,
    qkv_weight,
    qkv_bias,
    out_weight,
    out_bias,
    second_gain,
    second_shift,
    merge_weight,
    merge_bias,
    dest_device,
    dest_slot,
):
    tokens = patch_states.shape[0]
    width = D
    axes = ("fsdp", "dp")

    qkv_parts = lax.all_gather(qkv_weight, axes, axis=0, tiled=False)
    out_rows = out_weight.shape[0]
    merge_rows = merge_weight.shape[0]
    lanes = 128
    flat = jnp.concatenate(
        [out_weight.reshape(-1, lanes), merge_weight.reshape(-1, lanes)], axis=0
    )
    qkv_parts, flat = lax.optimization_barrier((qkv_parts, flat))
    rest = lax.all_gather(flat, axes, axis=0, tiled=False)
    devices = rest.shape[0]
    qkv_full = qkv_parts.reshape(devices * qkv_weight.shape[0], width)
    out_cut = out_rows * width // lanes
    out_full = rest[:, :out_cut].reshape(devices * out_rows, width)
    merge_full = rest[:, out_cut:].reshape(devices * merge_rows, 4 * width)

    normed = layer_norm(patch_states, first_gain, first_shift).astype(jnp.bfloat16)
    joined_t = lax.dot_general(
        qkv_full, normed, (((1,), (1,)), ((), ())), preferred_element_type=jnp.float32
    )
    joined_t = (joined_t + qkv_bias[:, None]).astype(jnp.bfloat16)

    attended_t = attention(joined_t, segment_ids, 1024)

    projected_att = lax.dot_general(
        attended_t, out_full, (((0,), (1,)), ((), ())), preferred_element_type=jnp.float32
    )
    hidden = (patch_states.astype(jnp.float32) + projected_att + out_bias).astype(
        jnp.bfloat16
    )
    merged = (
        layer_norm(hidden, second_gain, second_shift)
        .astype(jnp.bfloat16)
        .reshape(tokens // 4, 4 * width)
    )
    projected = (times_rows(merged, merge_full) + merge_bias).astype(jnp.bfloat16)

    fsdp_count = lax.axis_size("fsdp")
    dp_count = lax.axis_size("dp")
    count_dev = fsdp_count * dp_count
    row_count = tokens // 4
    capacity = 2 * (row_count // count_dev)
    matches = (dest_device[:, None] == jnp.arange(count_dev, dtype=jnp.int32)[None, :]).astype(
        jnp.int32
    )
    earlier = jnp.cumsum(matches, axis=0) - matches
    rank = jnp.sum(earlier * matches, axis=1)
    position = dest_device * capacity + rank
    lanes = 128
    slot_block = jnp.broadcast_to(dest_slot.astype(jnp.bfloat16)[:, None], (row_count, lanes))
    payload = jnp.concatenate([projected, slot_block], axis=1)
    place = (
        position[None, :] == jnp.arange(count_dev * capacity, dtype=jnp.int32)[:, None]
    ).astype(jnp.bfloat16)
    rows_out = jnp.dot(place, payload, preferred_element_type=jnp.float32)
    empty = (jnp.sum(place, axis=1, keepdims=True) == 0)
    slot_lane = jnp.where(empty, float(row_count), rows_out[:, width:])
    rows_out = jnp.concatenate([rows_out[:, :width], slot_lane], axis=1).astype(jnp.bfloat16)
    got = lax.all_to_all(
        rows_out.reshape(count_dev, capacity, width + lanes),
        axes,
        split_axis=0,
        concat_axis=0,
        tiled=True,
    ).reshape(count_dev * capacity, width + lanes)
    got_slots = got[:, width].astype(jnp.int32)
    pick = (
        got_slots[None, :] == jnp.arange(row_count, dtype=jnp.int32)[:, None]
    ).astype(jnp.bfloat16)
    requests = jnp.dot(pick, got[:, :width], preferred_element_type=jnp.float32).astype(
        jnp.bfloat16
    )
    return requests


def solution(mesh):
    in_specs = (
        P(("fsdp", "dp"), None),
        P(("fsdp", "dp")),
        P(),
        P(),
        P(("fsdp", "dp"), None),
        P(),
        P(("fsdp", "dp"), None),
        P(),
        P(),
        P(),
        P(("fsdp", "dp"), None),
        P(),
        P(("fsdp", "dp")),
        P(("fsdp", "dp")),
    )
    out_specs = P(("fsdp", "dp"), None)
    return jax.shard_map(
        per_device, mesh=mesh, in_specs=in_specs, out_specs=out_specs, check_vma=False
    )
```

```python
import functools
import math

import jax
import jax.numpy as jnp
from jax import lax
from jax.experimental import pallas as pl
from jax.experimental.pallas import tpu as pltpu
from jax.sharding import PartitionSpec as P

D = 1280
H = 16
HD = 80


EPSILON = 1e-06


def layer_norm(states, gain, shift):
    values = states.astype(jnp.float32)
    center = jnp.mean(values, axis=-1, keepdims=True)
    spread = jnp.mean(jnp.square(values - center), axis=-1, keepdims=True)
    return (values - center) * lax.rsqrt(spread + EPSILON) * gain + shift


def times_rows(left, piece):
    return lax.dot_general(
        left, piece, (((1,), (1,)), ((), ())), preferred_element_type=jnp.float32
    )


def attention_kernel(scale, q_ref, k_ref, v_ref, qid_ref, kid_ref, o_ref):
    q = q_ref[...]
    k = k_ref[...]
    v = v_ref[...]
    scores = lax.dot_general(
        q, k, (((0,), (0,)), ((), ())), preferred_element_type=jnp.float32
    )
    scores = scores * scale
    same = qid_ref[...] == kid_ref[...]
    masked = jnp.where(same, scores, -jnp.inf)
    top = jnp.max(masked, axis=-1, keepdims=True)
    expo = jnp.exp(masked - top)
    total = jnp.sum(expo, axis=-1, keepdims=True)
    probs = (expo / total).astype(jnp.bfloat16)
    out = lax.dot_general(
        v, probs, (((1,), (1,)), ((), ())), preferred_element_type=jnp.float32
    )
    o_ref[...] = out.astype(o_ref.dtype)


def attention(joined_t, segment_ids, block_q):
    tokens = joined_t.shape[1]
    scale = 1.0 / math.sqrt(HD)
    qid = segment_ids.reshape(tokens, 1)
    kid = segment_ids.reshape(1, tokens)
    flops = 4 * H * tokens * tokens * HD
    cost = pl.CostEstimate(
        flops=flops,
        transcendentals=H * tokens * tokens,
        bytes_accessed=joined_t.size * 2 + tokens * D * 2,
    )
    return pl.pallas_call(
        functools.partial(attention_kernel, scale),
        out_shape=jax.ShapeDtypeStruct((D, tokens), jnp.bfloat16),
        grid=(H, tokens // block_q),
        in_specs=[
            pl.BlockSpec((HD, block_q), lambda h, i: (h, i)),
            pl.BlockSpec((HD, tokens), lambda h, i: (H + h, 0)),
            pl.BlockSpec((HD, tokens), lambda h, i: (2 * H + h, 0)),
            pl.BlockSpec((block_q, 1), lambda h, i: (i, 0)),
            pl.BlockSpec((1, tokens), lambda h, i: (0, 0)),
        ],
        out_specs=pl.BlockSpec((HD, block_q), lambda h, i: (h, i)),
        cost_estimate=cost,
    )(joined_t, joined_t, joined_t, qid, kid)


def per_device(
    patch_states,
    segment_ids,
    first_gain,
    first_shift,
    qkv_weight,
    qkv_bias,
    out_weight,
    out_bias,
    second_gain,
    second_shift,
    merge_weight,
    merge_bias,
    dest_device,
    dest_slot,
):
    tokens = patch_states.shape[0]
    width = D
    axes = ("fsdp", "dp")

    qkv_rows = qkv_weight.shape[0]
    out_rows = out_weight.shape[0]
    merge_rows = merge_weight.shape[0]
    tile_rows = 16
    wide = 4 * width
    first = jnp.concatenate([qkv_weight, out_weight], axis=0)
    first_rows = first.shape[0]
    first_parts = lax.all_gather(first, axes, axis=0, tiled=True)
    merge_padded = jnp.concatenate(
        [merge_weight, jnp.zeros((tile_rows - merge_rows, wide), merge_weight.dtype)], axis=0
    )
    first_parts, merge_padded = lax.optimization_barrier((first_parts, merge_padded))
    merge_parts = lax.all_gather(merge_padded, axes, axis=0, tiled=True)
    devices = first_parts.shape[0] // first_rows
    device_base = jnp.arange(devices, dtype=jnp.int32)[:, None] * first_rows
    qkv_index = (device_base + jnp.arange(qkv_rows, dtype=jnp.int32)[None, :]).reshape(-1)
    out_index = (device_base + qkv_rows + jnp.arange(out_rows, dtype=jnp.int32)[None, :]).reshape(-1)
    qkv_full = jnp.take(first_parts, qkv_index, axis=0, unique_indices=True, indices_are_sorted=True)
    out_full = jnp.take(first_parts, out_index, axis=0, unique_indices=True, indices_are_sorted=True)
    merge_full = merge_parts

    normed = layer_norm(patch_states, first_gain, first_shift).astype(jnp.bfloat16)
    joined_t = lax.dot_general(
        qkv_full, normed, (((1,), (1,)), ((), ())), preferred_element_type=jnp.float32
    )
    joined_t = (joined_t + qkv_bias[:, None]).astype(jnp.bfloat16)

    attended_t = attention(joined_t, segment_ids, 1024)

    projected_att = lax.dot_general(
        attended_t, out_full, (((0,), (1,)), ((), ())), preferred_element_type=jnp.float32
    )
    hidden = (patch_states.astype(jnp.float32) + projected_att + out_bias).astype(
        jnp.bfloat16
    )
    merged = (
        layer_norm(hidden, second_gain, second_shift)
        .astype(jnp.bfloat16)
        .reshape(tokens // 4, 4 * width)
    )
    projected_padded = lax.optimization_barrier(times_rows(merged, merge_full))
    projected = projected_padded.reshape(tokens // 4, devices, tile_rows)[:, :, :merge_rows]
    projected = (projected.reshape(tokens // 4, width) + merge_bias).astype(jnp.bfloat16)

    fsdp_count = lax.axis_size("fsdp")
    dp_count = lax.axis_size("dp")
    count_dev = fsdp_count * dp_count
    row_count = tokens // 4
    capacity = 2 * (row_count // count_dev)
    matches = (dest_device[:, None] == jnp.arange(count_dev, dtype=jnp.int32)[None, :]).astype(
        jnp.int32
    )
    earlier = jnp.cumsum(matches, axis=0) - matches
    rank = jnp.sum(earlier * matches, axis=1)
    position = dest_device * capacity + rank
    lanes = 128
    slot_block = jnp.broadcast_to(dest_slot.astype(jnp.bfloat16)[:, None], (row_count, lanes))
    payload = jnp.concatenate([projected, slot_block], axis=1)
    place = (
        position[None, :] == jnp.arange(count_dev * capacity, dtype=jnp.int32)[:, None]
    ).astype(jnp.bfloat16)
    rows_out = jnp.dot(place, payload, preferred_element_type=jnp.float32)
    empty = (jnp.sum(place, axis=1, keepdims=True) == 0)
    slot_lane = jnp.where(empty, float(row_count), rows_out[:, width:])
    rows_out = jnp.concatenate([rows_out[:, :width], slot_lane], axis=1).astype(jnp.bfloat16)
    got = lax.all_to_all(
        rows_out.reshape(count_dev, capacity, width + lanes),
        axes,
        split_axis=0,
        concat_axis=0,
        tiled=True,
    ).reshape(count_dev * capacity, width + lanes)
    got_slots = got[:, width].astype(jnp.int32)
    pick = (
        got_slots[None, :] == jnp.arange(row_count, dtype=jnp.int32)[:, None]
    ).astype(jnp.bfloat16)
    requests = jnp.dot(pick, got[:, :width], preferred_element_type=jnp.float32).astype(
        jnp.bfloat16
    )
    return requests


def solution(mesh):
    in_specs = (
        P(("fsdp", "dp"), None),
        P(("fsdp", "dp")),
        P(),
        P(),
        P(("fsdp", "dp"), None),
        P(),
        P(("fsdp", "dp"), None),
        P(),
        P(),
        P(),
        P(("fsdp", "dp"), None),
        P(),
        P(("fsdp", "dp")),
        P(("fsdp", "dp")),
    )
    out_specs = P(("fsdp", "dp"), None)
    return jax.shard_map(
        per_device, mesh=mesh, in_specs=in_specs, out_specs=out_specs, check_vma=False
    )
```

```python
import functools
import math

import jax
import jax.numpy as jnp
from jax import lax
from jax.experimental import pallas as pl
from jax.experimental.pallas import tpu as pltpu
from jax.sharding import PartitionSpec as P

D = 1280
H = 16
HD = 80


EPSILON = 1e-06


def layer_norm(states, gain, shift):
    values = states.astype(jnp.float32)
    center = jnp.mean(values, axis=-1, keepdims=True)
    spread = jnp.mean(jnp.square(values - center), axis=-1, keepdims=True)
    return (values - center) * lax.rsqrt(spread + EPSILON) * gain + shift


def times_rows(left, piece):
    return lax.dot_general(
        left, piece, (((1,), (1,)), ((), ())), preferred_element_type=jnp.float32
    )


def attention_kernel(scale, q_ref, k_ref, v_ref, qid_ref, kid_ref, o_ref):
    q = q_ref[...]
    k = k_ref[...]
    v = v_ref[...]
    scores = lax.dot_general(
        q, k, (((0,), (0,)), ((), ())), preferred_element_type=jnp.float32
    )
    scores = scores * scale
    same = qid_ref[...] == kid_ref[...]
    masked = jnp.where(same, scores, -jnp.inf)
    top = jnp.max(masked, axis=-1, keepdims=True)
    expo = jnp.exp(masked - top)
    total = jnp.sum(expo, axis=-1, keepdims=True)
    probs = (expo / total).astype(jnp.bfloat16)
    out = lax.dot_general(
        v, probs, (((1,), (1,)), ((), ())), preferred_element_type=jnp.float32
    )
    o_ref[...] = out.astype(o_ref.dtype)


def attention(joined_t, segment_ids, block_q):
    tokens = joined_t.shape[1]
    scale = 1.0 / math.sqrt(HD)
    qid = segment_ids.reshape(tokens, 1)
    kid = segment_ids.reshape(1, tokens)
    flops = 4 * H * tokens * tokens * HD
    cost = pl.CostEstimate(
        flops=flops,
        transcendentals=H * tokens * tokens,
        bytes_accessed=joined_t.size * 2 + tokens * D * 2,
    )
    return pl.pallas_call(
        functools.partial(attention_kernel, scale),
        out_shape=jax.ShapeDtypeStruct((D, tokens), jnp.bfloat16),
        grid=(H, tokens // block_q),
        in_specs=[
            pl.BlockSpec((HD, block_q), lambda h, i: (h, i)),
            pl.BlockSpec((HD, tokens), lambda h, i: (H + h, 0)),
            pl.BlockSpec((HD, tokens), lambda h, i: (2 * H + h, 0)),
            pl.BlockSpec((block_q, 1), lambda h, i: (i, 0)),
            pl.BlockSpec((1, tokens), lambda h, i: (0, 0)),
        ],
        out_specs=pl.BlockSpec((HD, block_q), lambda h, i: (h, i)),
        cost_estimate=cost,
    )(joined_t, joined_t, joined_t, qid, kid)


def per_device(
    patch_states,
    segment_ids,
    first_gain,
    first_shift,
    qkv_weight,
    qkv_bias,
    out_weight,
    out_bias,
    second_gain,
    second_shift,
    merge_weight,
    merge_bias,
    dest_device,
    dest_slot,
):
    tokens = patch_states.shape[0]
    width = D
    axes = ("fsdp", "dp")

    qkv_rows = qkv_weight.shape[0]
    out_rows = out_weight.shape[0]
    merge_rows = merge_weight.shape[0]
    tile_rows = 16
    wide = 4 * width
    first = jnp.concatenate([qkv_weight, out_weight], axis=0)
    first_rows = first.shape[0]
    first_parts = lax.all_gather(first, axes, axis=0, tiled=True)
    merge_padded = jnp.concatenate(
        [merge_weight, jnp.zeros((tile_rows - merge_rows, wide), merge_weight.dtype)], axis=0
    )
    first_parts, merge_padded = lax.optimization_barrier((first_parts, merge_padded))
    merge_parts = lax.all_gather(merge_padded, axes, axis=0, tiled=True)
    devices = first_parts.shape[0] // first_rows
    group = 8
    blocks = first_parts.reshape(devices // group, group * first_rows, width)
    source = lax.broadcasted_iota(jnp.int32, (1, group * first_rows), 1)

    def selector(rows, offset):
        target = lax.broadcasted_iota(jnp.int32, (group * rows, 1), 0)
        wanted = (target // rows) * first_rows + offset + target % rows
        return (wanted == source).astype(first_parts.dtype)

    def pick(rows, offset):
        picked = jnp.einsum(
            "ij,bjk->bik", selector(rows, offset), blocks, preferred_element_type=jnp.float32
        )
        return picked.astype(first_parts.dtype).reshape(devices * rows, width)

    qkv_full = pick(qkv_rows, 0)
    out_full = pick(out_rows, qkv_rows)
    merge_full = merge_parts

    normed = layer_norm(patch_states, first_gain, first_shift).astype(jnp.bfloat16)
    joined_t = lax.dot_general(
        qkv_full, normed, (((1,), (1,)), ((), ())), preferred_element_type=jnp.float32
    )
    joined_t = (joined_t + qkv_bias[:, None]).astype(jnp.bfloat16)

    attended_t = attention(joined_t, segment_ids, 1024)

    projected_att = lax.dot_general(
        attended_t, out_full, (((0,), (1,)), ((), ())), preferred_element_type=jnp.float32
    )
    hidden = (patch_states.astype(jnp.float32) + projected_att + out_bias).astype(
        jnp.bfloat16
    )
    merged = (
        layer_norm(hidden, second_gain, second_shift)
        .astype(jnp.bfloat16)
        .reshape(tokens // 4, 4 * width)
    )
    projected_padded = lax.optimization_barrier(times_rows(merged, merge_full))
    projected = projected_padded.reshape(tokens // 4, devices, tile_rows)[:, :, :merge_rows]
    projected = (projected.reshape(tokens // 4, width) + merge_bias).astype(jnp.bfloat16)

    fsdp_count = lax.axis_size("fsdp")
    dp_count = lax.axis_size("dp")
    count_dev = fsdp_count * dp_count
    row_count = tokens // 4
    capacity = 2 * (row_count // count_dev)
    matches = (dest_device[:, None] == jnp.arange(count_dev, dtype=jnp.int32)[None, :]).astype(
        jnp.int32
    )
    earlier = jnp.cumsum(matches, axis=0) - matches
    rank = jnp.sum(earlier * matches, axis=1)
    position = dest_device * capacity + rank
    lanes = 128
    slot_block = jnp.broadcast_to(dest_slot.astype(jnp.bfloat16)[:, None], (row_count, lanes))
    payload = jnp.concatenate([projected, slot_block], axis=1)
    place = (
        position[None, :] == jnp.arange(count_dev * capacity, dtype=jnp.int32)[:, None]
    ).astype(jnp.bfloat16)
    rows_out = jnp.dot(place, payload, preferred_element_type=jnp.float32)
    empty = (jnp.sum(place, axis=1, keepdims=True) == 0)
    slot_lane = jnp.where(empty, float(row_count), rows_out[:, width:])
    rows_out = jnp.concatenate([rows_out[:, :width], slot_lane], axis=1).astype(jnp.bfloat16)
    got = lax.all_to_all(
        rows_out.reshape(count_dev, capacity, width + lanes),
        axes,
        split_axis=0,
        concat_axis=0,
        tiled=True,
    ).reshape(count_dev * capacity, width + lanes)
    got_slots = got[:, width].astype(jnp.int32)
    pick = (
        got_slots[None, :] == jnp.arange(row_count, dtype=jnp.int32)[:, None]
    ).astype(jnp.bfloat16)
    requests = jnp.dot(pick, got[:, :width], preferred_element_type=jnp.float32).astype(
        jnp.bfloat16
    )
    return requests


def solution(mesh):
    in_specs = (
        P(("fsdp", "dp"), None),
        P(("fsdp", "dp")),
        P(),
        P(),
        P(("fsdp", "dp"), None),
        P(),
        P(("fsdp", "dp"), None),
        P(),
        P(),
        P(),
        P(("fsdp", "dp"), None),
        P(),
        P(("fsdp", "dp")),
        P(("fsdp", "dp")),
    )
    out_specs = P(("fsdp", "dp"), None)
    return jax.shard_map(
        per_device, mesh=mesh, in_specs=in_specs, out_specs=out_specs, check_vma=False
    )
```

```python
import functools
import math

import jax
import jax.numpy as jnp
from jax import lax
from jax.experimental import pallas as pl
from jax.experimental.pallas import tpu as pltpu
from jax.sharding import PartitionSpec as P

D = 1280
H = 16
HD = 80


EPSILON = 1e-06


def layer_norm(states, gain, shift):
    values = states.astype(jnp.float32)
    center = jnp.mean(values, axis=-1, keepdims=True)
    spread = jnp.mean(jnp.square(values - center), axis=-1, keepdims=True)
    return (values - center) * lax.rsqrt(spread + EPSILON) * gain + shift


def times_rows(left, piece):
    return lax.dot_general(
        left, piece, (((1,), (1,)), ((), ())), preferred_element_type=jnp.float32
    )


def attention_kernel(scale, q_ref, k_ref, v_ref, qid_ref, kid_ref, o_ref):
    q = q_ref[...]
    k = k_ref[...]
    v = v_ref[...]
    scores = lax.dot_general(
        q, k, (((0,), (0,)), ((), ())), preferred_element_type=jnp.float32
    )
    scores = scores * scale
    same = qid_ref[...] == kid_ref[...]
    masked = jnp.where(same, scores, -jnp.inf)
    top = jnp.max(masked, axis=-1, keepdims=True)
    expo = jnp.exp(masked - top)
    total = jnp.sum(expo, axis=-1, keepdims=True)
    probs = (expo / total).astype(jnp.bfloat16)
    out = lax.dot_general(
        v, probs, (((1,), (1,)), ((), ())), preferred_element_type=jnp.float32
    )
    o_ref[...] = out.astype(o_ref.dtype)


def attention(joined_t, segment_ids, block_q):
    tokens = joined_t.shape[1]
    scale = 1.0 / math.sqrt(HD)
    qid = segment_ids.reshape(tokens, 1)
    kid = segment_ids.reshape(1, tokens)
    flops = 4 * H * tokens * tokens * HD
    cost = pl.CostEstimate(
        flops=flops,
        transcendentals=H * tokens * tokens,
        bytes_accessed=joined_t.size * 2 + tokens * D * 2,
    )
    return pl.pallas_call(
        functools.partial(attention_kernel, scale),
        out_shape=jax.ShapeDtypeStruct((D, tokens), jnp.bfloat16),
        grid=(H, tokens // block_q),
        in_specs=[
            pl.BlockSpec((HD, block_q), lambda h, i: (h, i)),
            pl.BlockSpec((HD, tokens), lambda h, i: (H + h, 0)),
            pl.BlockSpec((HD, tokens), lambda h, i: (2 * H + h, 0)),
            pl.BlockSpec((block_q, 1), lambda h, i: (i, 0)),
            pl.BlockSpec((1, tokens), lambda h, i: (0, 0)),
        ],
        out_specs=pl.BlockSpec((HD, block_q), lambda h, i: (h, i)),
        cost_estimate=cost,
    )(joined_t, joined_t, joined_t, qid, kid)


def per_device(
    patch_states,
    segment_ids,
    first_gain,
    first_shift,
    qkv_weight,
    qkv_bias,
    out_weight,
    out_bias,
    second_gain,
    second_shift,
    merge_weight,
    merge_bias,
    dest_device,
    dest_slot,
):
    tokens = patch_states.shape[0]
    width = D
    axes = ("fsdp", "dp")

    qkv_rows = qkv_weight.shape[0]
    out_rows = out_weight.shape[0]
    merge_rows = merge_weight.shape[0]
    tile_rows = 16
    wide = 4 * width
    first = jnp.concatenate([qkv_weight, out_weight], axis=0)
    first_rows = first.shape[0]
    first_parts = lax.all_gather(first, axes, axis=0, tiled=True)
    merge_padded = jnp.concatenate(
        [merge_weight, jnp.zeros((tile_rows - merge_rows, wide), merge_weight.dtype)], axis=0
    )
    first_parts, merge_padded = lax.optimization_barrier((first_parts, merge_padded))
    merge_parts = lax.all_gather(merge_padded, axes, axis=0, tiled=True)
    devices = first_parts.shape[0] // first_rows
    group = 8
    blocks = first_parts.reshape(devices // group, group * first_rows, width)
    source = lax.broadcasted_iota(jnp.int32, (1, group * first_rows), 1)

    def selector(rows, offset):
        target = lax.broadcasted_iota(jnp.int32, (group * rows, 1), 0)
        wanted = (target // rows) * first_rows + offset + target % rows
        return (wanted == source).astype(first_parts.dtype)

    def pick(rows, offset):
        picked = jnp.einsum(
            "ij,bjk->bik", selector(rows, offset), blocks, preferred_element_type=jnp.float32
        )
        return picked.astype(first_parts.dtype).reshape(devices * rows, width)

    qkv_full = pick(qkv_rows, 0)
    out_full = pick(out_rows, qkv_rows)
    merge_full = merge_parts

    normed = layer_norm(patch_states, first_gain, first_shift).astype(jnp.bfloat16)
    joined_t = lax.dot_general(
        qkv_full, normed, (((1,), (1,)), ((), ())), preferred_element_type=jnp.float32
    )
    joined_t = (joined_t + qkv_bias[:, None]).astype(jnp.bfloat16)

    attended_t = attention(joined_t, segment_ids, 1024)

    projected_att = lax.dot_general(
        attended_t, out_full, (((0,), (1,)), ((), ())), preferred_element_type=jnp.float32
    )
    hidden = (patch_states.astype(jnp.float32) + projected_att + out_bias).astype(
        jnp.bfloat16
    )
    merged = (
        layer_norm(hidden, second_gain, second_shift)
        .astype(jnp.bfloat16)
        .reshape(tokens // 4, 4 * width)
    )
    projected_padded = lax.optimization_barrier(times_rows(merged, merge_full))
    projected = projected_padded.reshape(tokens // 4, devices, tile_rows)[:, :, :merge_rows]
    projected = (projected.reshape(tokens // 4, width) + merge_bias).astype(jnp.bfloat16)

    fsdp_count = lax.axis_size("fsdp")
    dp_count = lax.axis_size("dp")
    count_dev = fsdp_count * dp_count
    row_count = tokens // 4
    capacity = 2 * (row_count // count_dev)
    matches = (dest_device[:, None] == jnp.arange(count_dev, dtype=jnp.int32)[None, :]).astype(
        jnp.int32
    )
    earlier = jnp.cumsum(matches, axis=0) - matches
    rank = jnp.sum(earlier * matches, axis=1)
    position = dest_device * capacity + rank
    lanes = 128
    slot_block = jnp.broadcast_to(dest_slot.astype(jnp.bfloat16)[:, None], (row_count, lanes))
    payload = jnp.concatenate([projected, slot_block], axis=1)
    place = (
        position[None, :] == jnp.arange(count_dev * capacity, dtype=jnp.int32)[:, None]
    ).astype(jnp.bfloat16)
    rows_out = jnp.dot(place, payload, preferred_element_type=jnp.float32)
    empty = (jnp.sum(place, axis=1, keepdims=True) == 0)
    slot_lane = jnp.where(empty, float(row_count), rows_out[:, width:])
    rows_out = jnp.concatenate([rows_out[:, :width], slot_lane], axis=1).astype(jnp.bfloat16)
    staged = rows_out.reshape(fsdp_count, dp_count, capacity, width + lanes)
    staged = lax.all_to_all(staged, "dp", split_axis=1, concat_axis=1, tiled=True)
    staged = lax.all_to_all(staged, "fsdp", split_axis=0, concat_axis=0, tiled=True)
    got = staged.reshape(count_dev * capacity, width + lanes)
    got_slots = got[:, width].astype(jnp.int32)
    pick = (
        got_slots[None, :] == jnp.arange(row_count, dtype=jnp.int32)[:, None]
    ).astype(jnp.bfloat16)
    requests = jnp.dot(pick, got[:, :width], preferred_element_type=jnp.float32).astype(
        jnp.bfloat16
    )
    return requests


def solution(mesh):
    in_specs = (
        P(("fsdp", "dp"), None),
        P(("fsdp", "dp")),
        P(),
        P(),
        P(("fsdp", "dp"), None),
        P(),
        P(("fsdp", "dp"), None),
        P(),
        P(),
        P(),
        P(("fsdp", "dp"), None),
        P(),
        P(("fsdp", "dp")),
        P(("fsdp", "dp")),
    )
    out_specs = P(("fsdp", "dp"), None)
    return jax.shard_map(
        per_device, mesh=mesh, in_specs=in_specs, out_specs=out_specs, check_vma=False
    )
```

```python
import functools
import math

import jax
import jax.numpy as jnp
from jax import lax
from jax.experimental import pallas as pl
from jax.experimental.pallas import tpu as pltpu
from jax.sharding import PartitionSpec as P

D = 1280
H = 16
HD = 80


EPSILON = 1e-06


def layer_norm(states, gain, shift):
    values = states.astype(jnp.float32)
    center = jnp.mean(values, axis=-1, keepdims=True)
    spread = jnp.mean(jnp.square(values - center), axis=-1, keepdims=True)
    return (values - center) * lax.rsqrt(spread + EPSILON) * gain + shift


def times_rows(left, piece):
    return lax.dot_general(
        left, piece, (((1,), (1,)), ((), ())), preferred_element_type=jnp.float32
    )


def attention_kernel(scale, q_ref, k_ref, v_ref, qid_ref, kid_ref, o_ref):
    q = q_ref[...]
    k = k_ref[...]
    v = v_ref[...]
    scores = lax.dot_general(
        q, k, (((0,), (0,)), ((), ())), preferred_element_type=jnp.float32
    )
    scores = scores * scale
    same = qid_ref[...] == kid_ref[...]
    masked = jnp.where(same, scores, -jnp.inf)
    top = jnp.max(masked, axis=-1, keepdims=True)
    expo = jnp.exp(masked - top)
    total = jnp.sum(expo, axis=-1, keepdims=True)
    probs = (expo / total).astype(jnp.bfloat16)
    out = lax.dot_general(
        v, probs, (((1,), (1,)), ((), ())), preferred_element_type=jnp.float32
    )
    o_ref[...] = out.astype(o_ref.dtype)


def attention(joined_t, segment_ids, block_q):
    tokens = joined_t.shape[1]
    scale = 1.0 / math.sqrt(HD)
    qid = segment_ids.reshape(tokens, 1)
    kid = segment_ids.reshape(1, tokens)
    flops = 4 * H * tokens * tokens * HD
    cost = pl.CostEstimate(
        flops=flops,
        transcendentals=H * tokens * tokens,
        bytes_accessed=joined_t.size * 2 + tokens * D * 2,
    )
    return pl.pallas_call(
        functools.partial(attention_kernel, scale),
        out_shape=jax.ShapeDtypeStruct((D, tokens), jnp.bfloat16),
        grid=(H, tokens // block_q),
        in_specs=[
            pl.BlockSpec((HD, block_q), lambda h, i: (h, i)),
            pl.BlockSpec((HD, tokens), lambda h, i: (H + h, 0)),
            pl.BlockSpec((HD, tokens), lambda h, i: (2 * H + h, 0)),
            pl.BlockSpec((block_q, 1), lambda h, i: (i, 0)),
            pl.BlockSpec((1, tokens), lambda h, i: (0, 0)),
        ],
        out_specs=pl.BlockSpec((HD, block_q), lambda h, i: (h, i)),
        cost_estimate=cost,
    )(joined_t, joined_t, joined_t, qid, kid)


def per_device(
    patch_states,
    segment_ids,
    first_gain,
    first_shift,
    qkv_weight,
    qkv_bias,
    out_weight,
    out_bias,
    second_gain,
    second_shift,
    merge_weight,
    merge_bias,
    dest_device,
    dest_slot,
):
    tokens = patch_states.shape[0]
    width = D
    axes = ("fsdp", "dp")

    qkv_rows = qkv_weight.shape[0]
    out_rows = out_weight.shape[0]
    merge_rows = merge_weight.shape[0]
    tile_rows = 16
    wide = 4 * width
    first = jnp.concatenate([qkv_weight, out_weight], axis=0)
    first_rows = first.shape[0]
    first_parts = lax.all_gather(first, axes, axis=0, tiled=True)
    merge_padded = jnp.concatenate(
        [merge_weight, jnp.zeros((tile_rows - merge_rows, wide), merge_weight.dtype)], axis=0
    )
    merge_parts = lax.all_gather(merge_padded, axes, axis=0, tiled=True)
    devices = first_parts.shape[0] // first_rows
    group = 8
    blocks = first_parts.reshape(devices // group, group * first_rows, width)
    source = lax.broadcasted_iota(jnp.int32, (1, group * first_rows), 1)

    def selector(rows, offset):
        target = lax.broadcasted_iota(jnp.int32, (group * rows, 1), 0)
        wanted = (target // rows) * first_rows + offset + target % rows
        return (wanted == source).astype(first_parts.dtype)

    def pick(rows, offset):
        picked = jnp.einsum(
            "ij,bjk->bik", selector(rows, offset), blocks, preferred_element_type=jnp.float32
        )
        return picked.astype(first_parts.dtype).reshape(devices * rows, width)

    qkv_full = pick(qkv_rows, 0)
    out_full = pick(out_rows, qkv_rows)
    merge_full = merge_parts

    normed = layer_norm(patch_states, first_gain, first_shift).astype(jnp.bfloat16)
    joined_t = lax.dot_general(
        qkv_full, normed, (((1,), (1,)), ((), ())), preferred_element_type=jnp.float32
    )
    joined_t = (joined_t + qkv_bias[:, None]).astype(jnp.bfloat16)

    attended_t = attention(joined_t, segment_ids, 1024)

    projected_att = lax.dot_general(
        attended_t, out_full, (((0,), (1,)), ((), ())), preferred_element_type=jnp.float32
    )
    hidden = (patch_states.astype(jnp.float32) + projected_att + out_bias).astype(
        jnp.bfloat16
    )
    merged = (
        layer_norm(hidden, second_gain, second_shift)
        .astype(jnp.bfloat16)
        .reshape(tokens // 4, 4 * width)
    )
    projected_padded = lax.optimization_barrier(times_rows(merged, merge_full))
    projected = projected_padded.reshape(tokens // 4, devices, tile_rows)[:, :, :merge_rows]
    projected = (projected.reshape(tokens // 4, width) + merge_bias).astype(jnp.bfloat16)

    fsdp_count = lax.axis_size("fsdp")
    dp_count = lax.axis_size("dp")
    count_dev = fsdp_count * dp_count
    row_count = tokens // 4
    capacity = 2 * (row_count // count_dev)
    matches = (dest_device[:, None] == jnp.arange(count_dev, dtype=jnp.int32)[None, :]).astype(
        jnp.int32
    )
    earlier = jnp.cumsum(matches, axis=0) - matches
    rank = jnp.sum(earlier * matches, axis=1)
    position = dest_device * capacity + rank
    lanes = 128
    slot_block = jnp.broadcast_to(dest_slot.astype(jnp.bfloat16)[:, None], (row_count, lanes))
    payload = jnp.concatenate([projected, slot_block], axis=1)
    place = (
        position[None, :] == jnp.arange(count_dev * capacity, dtype=jnp.int32)[:, None]
    ).astype(jnp.bfloat16)
    rows_out = jnp.dot(place, payload, preferred_element_type=jnp.float32)
    empty = (jnp.sum(place, axis=1, keepdims=True) == 0)
    slot_lane = jnp.where(empty, float(row_count), rows_out[:, width:])
    rows_out = jnp.concatenate([rows_out[:, :width], slot_lane], axis=1).astype(jnp.bfloat16)
    got = lax.all_to_all(
        rows_out.reshape(count_dev, capacity, width + lanes),
        axes,
        split_axis=0,
        concat_axis=0,
        tiled=True,
    ).reshape(count_dev * capacity, width + lanes)
    got_slots = got[:, width].astype(jnp.int32)
    pick = (
        got_slots[None, :] == jnp.arange(row_count, dtype=jnp.int32)[:, None]
    ).astype(jnp.bfloat16)
    requests = jnp.dot(pick, got[:, :width], preferred_element_type=jnp.float32).astype(
        jnp.bfloat16
    )
    return requests


def solution(mesh):
    in_specs = (
        P(("fsdp", "dp"), None),
        P(("fsdp", "dp")),
        P(),
        P(),
        P(("fsdp", "dp"), None),
        P(),
        P(("fsdp", "dp"), None),
        P(),
        P(),
        P(),
        P(("fsdp", "dp"), None),
        P(),
        P(("fsdp", "dp")),
        P(("fsdp", "dp")),
    )
    out_specs = P(("fsdp", "dp"), None)
    return jax.shard_map(
        per_device, mesh=mesh, in_specs=in_specs, out_specs=out_specs, check_vma=False
    )
```

```python
import functools
import math

import jax
import jax.numpy as jnp
from jax import lax
from jax.experimental import pallas as pl
from jax.experimental.pallas import tpu as pltpu
from jax.sharding import PartitionSpec as P

D = 1280
H = 16
HD = 80


EPSILON = 1e-06


def layer_norm(states, gain, shift):
    values = states.astype(jnp.float32)
    center = jnp.mean(values, axis=-1, keepdims=True)
    spread = jnp.mean(jnp.square(values - center), axis=-1, keepdims=True)
    return (values - center) * lax.rsqrt(spread + EPSILON) * gain + shift


def times_rows(left, piece):
    return lax.dot_general(
        left, piece, (((1,), (1,)), ((), ())), preferred_element_type=jnp.float32
    )


def attention_kernel(scale, q_ref, k_ref, v_ref, qid_ref, kid_ref, o_ref):
    q = q_ref[...]
    k = k_ref[...]
    v = v_ref[...]
    scores = lax.dot_general(
        q, k, (((0,), (0,)), ((), ())), preferred_element_type=jnp.float32
    )
    scores = scores * scale
    same = qid_ref[...] == kid_ref[...]
    masked = jnp.where(same, scores, -jnp.inf)
    top = jnp.max(masked, axis=-1, keepdims=True)
    expo = jnp.exp(masked - top)
    total = jnp.sum(expo, axis=-1, keepdims=True)
    probs = (expo / total).astype(jnp.bfloat16)
    out = lax.dot_general(
        v, probs, (((1,), (1,)), ((), ())), preferred_element_type=jnp.float32
    )
    o_ref[...] = out.astype(o_ref.dtype)


def attention(joined_t, segment_ids, block_q):
    tokens = joined_t.shape[1]
    scale = 1.0 / math.sqrt(HD)
    qid = segment_ids.reshape(tokens, 1)
    kid = segment_ids.reshape(1, tokens)
    flops = 4 * H * tokens * tokens * HD
    cost = pl.CostEstimate(
        flops=flops,
        transcendentals=H * tokens * tokens,
        bytes_accessed=joined_t.size * 2 + tokens * D * 2,
    )
    return pl.pallas_call(
        functools.partial(attention_kernel, scale),
        out_shape=jax.ShapeDtypeStruct((D, tokens), jnp.bfloat16),
        grid=(H, tokens // block_q),
        in_specs=[
            pl.BlockSpec((HD, block_q), lambda h, i: (h, i)),
            pl.BlockSpec((HD, tokens), lambda h, i: (H + h, 0)),
            pl.BlockSpec((HD, tokens), lambda h, i: (2 * H + h, 0)),
            pl.BlockSpec((block_q, 1), lambda h, i: (i, 0)),
            pl.BlockSpec((1, tokens), lambda h, i: (0, 0)),
        ],
        out_specs=pl.BlockSpec((HD, block_q), lambda h, i: (h, i)),
        cost_estimate=cost,
    )(joined_t, joined_t, joined_t, qid, kid)


def per_device(
    patch_states,
    segment_ids,
    first_gain,
    first_shift,
    qkv_weight,
    qkv_bias,
    out_weight,
    out_bias,
    second_gain,
    second_shift,
    merge_weight,
    merge_bias,
    dest_device,
    dest_slot,
):
    tokens = patch_states.shape[0]
    width = D
    axes = ("fsdp", "dp")

    qkv_rows = qkv_weight.shape[0]
    out_rows = out_weight.shape[0]
    merge_rows = merge_weight.shape[0]
    tile_rows = 16
    wide = 4 * width
    first = jnp.concatenate([qkv_weight, out_weight], axis=0)
    first_rows = first.shape[0]
    first_parts = lax.all_gather(first, axes, axis=0, tiled=True)
    merge_padded = jnp.concatenate(
        [merge_weight, jnp.zeros((tile_rows - merge_rows, wide), merge_weight.dtype)], axis=0
    )
    merge_parts = lax.all_gather(merge_padded, axes, axis=0, tiled=True)
    devices = first_parts.shape[0] // first_rows
    group = 8
    blocks = first_parts.reshape(devices // group, group * first_rows, width)
    source = lax.broadcasted_iota(jnp.int32, (1, group * first_rows), 1)

    def selector(rows, offset):
        target = lax.broadcasted_iota(jnp.int32, (group * rows, 1), 0)
        wanted = (target // rows) * first_rows + offset + target % rows
        return (wanted == source).astype(first_parts.dtype)

    def pick(rows, offset):
        picked = jnp.einsum(
            "ij,bjk->bik", selector(rows, offset), blocks, preferred_element_type=jnp.float32
        )
        return picked.astype(first_parts.dtype).reshape(devices * rows, width)

    qkv_full = pick(qkv_rows, 0)
    out_full = pick(out_rows, qkv_rows)
    merge_full = merge_parts

    normed = layer_norm(patch_states, first_gain, first_shift).astype(jnp.bfloat16)
    joined_t = lax.dot_general(
        qkv_full, normed, (((1,), (1,)), ((), ())), preferred_element_type=jnp.float32
    )
    joined_t = (joined_t + qkv_bias[:, None]).astype(jnp.bfloat16)

    attended_t = attention(joined_t, segment_ids, 1024)

    projected_att = lax.dot_general(
        attended_t, out_full, (((0,), (1,)), ((), ())), preferred_element_type=jnp.float32
    )
    hidden = (patch_states.astype(jnp.float32) + projected_att + out_bias).astype(
        jnp.bfloat16
    )
    merged = (
        layer_norm(hidden, second_gain, second_shift)
        .astype(jnp.bfloat16)
        .reshape(tokens // 4, 4 * width)
    )
    projected_padded = lax.optimization_barrier(times_rows(merged, merge_full))
    projected = projected_padded.reshape(tokens // 4, devices, tile_rows)[:, :, :merge_rows]
    projected = (projected.reshape(tokens // 4, width) + merge_bias).astype(jnp.bfloat16)

    fsdp_count = lax.axis_size("fsdp")
    dp_count = lax.axis_size("dp")
    count_dev = fsdp_count * dp_count
    row_count = tokens // 4
    capacity = 2 * (row_count // count_dev)
    matches = (dest_device[:, None] == jnp.arange(count_dev, dtype=jnp.int32)[None, :]).astype(
        jnp.int32
    )
    earlier = jnp.cumsum(matches, axis=0) - matches
    rank = jnp.sum(earlier * matches, axis=1)
    position = dest_device * capacity + rank
    place = (
        position[None, :] == jnp.arange(count_dev * capacity, dtype=jnp.int32)[:, None]
    ).astype(jnp.bfloat16)
    empty = jnp.sum(place, axis=1) == 0
    slot_sent = jnp.where(
        empty, row_count, jnp.sum(place.astype(jnp.int32) * dest_slot[None, :], axis=1)
    )
    got_slots = lax.all_to_all(
        slot_sent.reshape(count_dev, capacity), axes, split_axis=0, concat_axis=0, tiled=True
    ).reshape(-1)
    rows_out = jnp.dot(place, projected, preferred_element_type=jnp.float32).astype(jnp.bfloat16)
    got = lax.all_to_all(
        rows_out.reshape(count_dev, capacity, width), axes, split_axis=0, concat_axis=0, tiled=True
    ).reshape(count_dev * capacity, width)
    pick = (
        got_slots[None, :] == jnp.arange(row_count, dtype=jnp.int32)[:, None]
    ).astype(jnp.bfloat16)
    requests = jnp.dot(pick, got, preferred_element_type=jnp.float32).astype(jnp.bfloat16)
    return requests


def solution(mesh):
    in_specs = (
        P(("fsdp", "dp"), None),
        P(("fsdp", "dp")),
        P(),
        P(),
        P(("fsdp", "dp"), None),
        P(),
        P(("fsdp", "dp"), None),
        P(),
        P(),
        P(),
        P(("fsdp", "dp"), None),
        P(),
        P(("fsdp", "dp")),
        P(("fsdp", "dp")),
    )
    out_specs = P(("fsdp", "dp"), None)
    return jax.shard_map(
        per_device, mesh=mesh, in_specs=in_specs, out_specs=out_specs, check_vma=False
    )
```

```python
import functools
import math

import jax
import jax.numpy as jnp
from jax import lax
from jax.experimental import pallas as pl
from jax.experimental.pallas import tpu as pltpu
from jax.sharding import PartitionSpec as P

D = 1280
H = 16
HD = 80


EPSILON = 1e-06


def layer_norm(states, gain, shift):
    values = states.astype(jnp.float32)
    center = jnp.mean(values, axis=-1, keepdims=True)
    spread = jnp.mean(jnp.square(values - center), axis=-1, keepdims=True)
    return (values - center) * lax.rsqrt(spread + EPSILON) * gain + shift


def times_rows(left, piece):
    return lax.dot_general(
        left, piece, (((1,), (1,)), ((), ())), preferred_element_type=jnp.float32
    )


def attention_kernel(scale, q_ref, k_ref, v_ref, qid_ref, kid_ref, o_ref):
    q = q_ref[...]
    k = k_ref[...]
    v = v_ref[...]
    scores = lax.dot_general(
        q, k, (((0,), (0,)), ((), ())), preferred_element_type=jnp.float32
    )
    scores = scores * scale
    same = qid_ref[...] == kid_ref[...]
    masked = jnp.where(same, scores, -jnp.inf)
    top = jnp.max(masked, axis=-1, keepdims=True)
    expo = jnp.exp(masked - top)
    total = jnp.sum(expo, axis=-1, keepdims=True)
    probs = (expo / total).astype(jnp.bfloat16)
    out = lax.dot_general(
        v, probs, (((1,), (1,)), ((), ())), preferred_element_type=jnp.float32
    )
    o_ref[...] = out.astype(o_ref.dtype)


def attention(joined_t, segment_ids, block_q):
    tokens = joined_t.shape[1]
    scale = 1.0 / math.sqrt(HD)
    qid = segment_ids.reshape(tokens, 1)
    kid = segment_ids.reshape(1, tokens)
    flops = 4 * H * tokens * tokens * HD
    cost = pl.CostEstimate(
        flops=flops,
        transcendentals=H * tokens * tokens,
        bytes_accessed=joined_t.size * 2 + tokens * D * 2,
    )
    return pl.pallas_call(
        functools.partial(attention_kernel, scale),
        out_shape=jax.ShapeDtypeStruct((D, tokens), jnp.bfloat16),
        grid=(H, tokens // block_q),
        in_specs=[
            pl.BlockSpec((HD, block_q), lambda h, i: (h, i)),
            pl.BlockSpec((HD, tokens), lambda h, i: (H + h, 0)),
            pl.BlockSpec((HD, tokens), lambda h, i: (2 * H + h, 0)),
            pl.BlockSpec((block_q, 1), lambda h, i: (i, 0)),
            pl.BlockSpec((1, tokens), lambda h, i: (0, 0)),
        ],
        out_specs=pl.BlockSpec((HD, block_q), lambda h, i: (h, i)),
        cost_estimate=cost,
    )(joined_t, joined_t, joined_t, qid, kid)


def per_device(
    patch_states,
    segment_ids,
    first_gain,
    first_shift,
    qkv_weight,
    qkv_bias,
    out_weight,
    out_bias,
    second_gain,
    second_shift,
    merge_weight,
    merge_bias,
    dest_device,
    dest_slot,
):
    tokens = patch_states.shape[0]
    width = D
    axes = ("fsdp", "dp")

    qkv_rows = qkv_weight.shape[0]
    out_rows = out_weight.shape[0]
    merge_rows = merge_weight.shape[0]
    merge_head = (merge_rows // 8) * 8
    merge_tail = merge_rows - merge_head
    pieces = 4
    tail_rows = merge_tail * pieces
    first = jnp.concatenate(
        [qkv_weight, out_weight, merge_weight[merge_head:].reshape(tail_rows, width)], axis=0
    )
    first_rows = first.shape[0]
    first_parts = lax.all_gather(first, axes, axis=0, tiled=True)
    merge_full = lax.all_gather(merge_weight[:merge_head], axes, axis=0, tiled=True)
    devices = first_parts.shape[0] // first_rows
    group = 8
    blocks = first_parts.reshape(devices // group, group * first_rows, width)
    source = lax.broadcasted_iota(jnp.int32, (1, group * first_rows), 1)

    def selector(rows, offset):
        target = lax.broadcasted_iota(jnp.int32, (group * rows, 1), 0)
        wanted = (target // rows) * first_rows + offset + target % rows
        return (wanted == source).astype(first_parts.dtype)

    def pick(rows, offset):
        picked = jnp.einsum(
            "ij,bjk->bik", selector(rows, offset), blocks, preferred_element_type=jnp.float32
        )
        return picked.astype(first_parts.dtype).reshape(devices * rows, width)

    qkv_full = pick(qkv_rows, 0)
    out_full = pick(out_rows, qkv_rows)
    piece = lax.broadcasted_iota(jnp.int32, (pieces, group * merge_tail, 1), 0)
    local = lax.broadcasted_iota(jnp.int32, (pieces, group * merge_tail, 1), 1)
    wanted = (
        (local // merge_tail) * first_rows
        + qkv_rows
        + out_rows
        + pieces * (local % merge_tail)
        + piece
    )
    tail_select = (wanted == source[None]).astype(first_parts.dtype)
    tail_full = jnp.einsum(
        "jis,bsk->jbik", tail_select, blocks, preferred_element_type=jnp.float32
    ).astype(first_parts.dtype).reshape(pieces, devices * merge_tail, width)

    normed = layer_norm(patch_states, first_gain, first_shift).astype(jnp.bfloat16)
    joined_t = lax.dot_general(
        qkv_full, normed, (((1,), (1,)), ((), ())), preferred_element_type=jnp.float32
    )
    joined_t = (joined_t + qkv_bias[:, None]).astype(jnp.bfloat16)

    attended_t = attention(joined_t, segment_ids, 1024)

    projected_att = lax.dot_general(
        attended_t, out_full, (((0,), (1,)), ((), ())), preferred_element_type=jnp.float32
    )
    hidden = (patch_states.astype(jnp.float32) + projected_att + out_bias).astype(
        jnp.bfloat16
    )
    merged = (
        layer_norm(hidden, second_gain, second_shift)
        .astype(jnp.bfloat16)
        .reshape(tokens // 4, 4 * width)
    )
    head_part = lax.optimization_barrier(times_rows(merged, merge_full))
    head_part = head_part.reshape(tokens // 4, devices, merge_head)
    tail_part = lax.optimization_barrier(
        jnp.einsum(
            "mjc,joc->mo",
            merged.reshape(tokens // 4, pieces, width),
            tail_full,
            preferred_element_type=jnp.float32,
        )
    ).reshape(tokens // 4, devices, merge_tail)
    projected = jnp.concatenate([head_part, tail_part], axis=2).reshape(tokens // 4, width)
    projected = (projected + merge_bias).astype(jnp.bfloat16)

    fsdp_count = lax.axis_size("fsdp")
    dp_count = lax.axis_size("dp")
    count_dev = fsdp_count * dp_count
    row_count = tokens // 4
    capacity = 2 * (row_count // count_dev)
    matches = (dest_device[:, None] == jnp.arange(count_dev, dtype=jnp.int32)[None, :]).astype(
        jnp.int32
    )
    earlier = jnp.cumsum(matches, axis=0) - matches
    rank = jnp.sum(earlier * matches, axis=1)
    position = dest_device * capacity + rank
    place = (
        position[None, :] == jnp.arange(count_dev * capacity, dtype=jnp.int32)[:, None]
    ).astype(jnp.bfloat16)
    empty = jnp.sum(place, axis=1) == 0
    slot_sent = jnp.where(
        empty, row_count, jnp.sum(place.astype(jnp.int32) * dest_slot[None, :], axis=1)
    )
    got_slots = lax.all_to_all(
        slot_sent.reshape(count_dev, capacity), axes, split_axis=0, concat_axis=0, tiled=True
    ).reshape(-1)
    rows_out = jnp.dot(place, projected, preferred_element_type=jnp.float32).astype(jnp.bfloat16)
    got = lax.all_to_all(
        rows_out.reshape(count_dev, capacity, width), axes, split_axis=0, concat_axis=0, tiled=True
    ).reshape(count_dev * capacity, width)
    pick = (
        got_slots[None, :] == jnp.arange(row_count, dtype=jnp.int32)[:, None]
    ).astype(jnp.bfloat16)
    requests = jnp.dot(pick, got, preferred_element_type=jnp.float32).astype(jnp.bfloat16)
    return requests


def solution(mesh):
    in_specs = (
        P(("fsdp", "dp"), None),
        P(("fsdp", "dp")),
        P(),
        P(),
        P(("fsdp", "dp"), None),
        P(),
        P(("fsdp", "dp"), None),
        P(),
        P(),
        P(),
        P(("fsdp", "dp"), None),
        P(),
        P(("fsdp", "dp")),
        P(("fsdp", "dp")),
    )
    out_specs = P(("fsdp", "dp"), None)
    return jax.shard_map(
        per_device, mesh=mesh, in_specs=in_specs, out_specs=out_specs, check_vma=False
    )
```

```python
import functools
import math

import jax
import jax.numpy as jnp
from jax import lax
from jax.experimental import pallas as pl
from jax.experimental.pallas import tpu as pltpu
from jax.sharding import PartitionSpec as P

D = 1280
H = 16
HD = 80


EPSILON = 1e-06


def layer_norm(states, gain, shift):
    values = states.astype(jnp.float32)
    center = jnp.mean(values, axis=-1, keepdims=True)
    spread = jnp.mean(jnp.square(values - center), axis=-1, keepdims=True)
    return (values - center) * lax.rsqrt(spread + EPSILON) * gain + shift


def times_rows(left, piece):
    return lax.dot_general(
        left, piece, (((1,), (1,)), ((), ())), preferred_element_type=jnp.float32
    )


def attention_kernel(scale, q_ref, k_ref, v_ref, qid_ref, kid_ref, o_ref):
    q = q_ref[...]
    k = k_ref[...]
    v = v_ref[...]
    scores = lax.dot_general(
        q, k, (((0,), (0,)), ((), ())), preferred_element_type=jnp.float32
    )
    scores = scores * scale
    same = qid_ref[...] == kid_ref[...]
    masked = jnp.where(same, scores, -jnp.inf)
    top = jnp.max(masked, axis=-1, keepdims=True)
    expo = jnp.exp(masked - top)
    total = jnp.sum(expo, axis=-1, keepdims=True)
    probs = (expo / total).astype(jnp.bfloat16)
    out = lax.dot_general(
        v, probs, (((1,), (1,)), ((), ())), preferred_element_type=jnp.float32
    )
    o_ref[...] = out.astype(o_ref.dtype)


def attention(joined_t, segment_ids, block_q):
    tokens = joined_t.shape[1]
    scale = 1.0 / math.sqrt(HD)
    qid = segment_ids.reshape(tokens, 1)
    kid = segment_ids.reshape(1, tokens)
    flops = 4 * H * tokens * tokens * HD
    cost = pl.CostEstimate(
        flops=flops,
        transcendentals=H * tokens * tokens,
        bytes_accessed=joined_t.size * 2 + tokens * D * 2,
    )
    return pl.pallas_call(
        functools.partial(attention_kernel, scale),
        out_shape=jax.ShapeDtypeStruct((D, tokens), jnp.bfloat16),
        grid=(H, tokens // block_q),
        in_specs=[
            pl.BlockSpec((HD, block_q), lambda h, i: (h, i)),
            pl.BlockSpec((HD, tokens), lambda h, i: (H + h, 0)),
            pl.BlockSpec((HD, tokens), lambda h, i: (2 * H + h, 0)),
            pl.BlockSpec((block_q, 1), lambda h, i: (i, 0)),
            pl.BlockSpec((1, tokens), lambda h, i: (0, 0)),
        ],
        out_specs=pl.BlockSpec((HD, block_q), lambda h, i: (h, i)),
        cost_estimate=cost,
    )(joined_t, joined_t, joined_t, qid, kid)


def per_device(
    patch_states,
    segment_ids,
    first_gain,
    first_shift,
    qkv_weight,
    qkv_bias,
    out_weight,
    out_bias,
    second_gain,
    second_shift,
    merge_weight,
    merge_bias,
    dest_device,
    dest_slot,
):
    tokens = patch_states.shape[0]
    width = D
    axes = ("fsdp", "dp")

    qkv_rows = qkv_weight.shape[0]
    out_rows = out_weight.shape[0]
    merge_rows = merge_weight.shape[0]
    tile_rows = 16
    wide = 4 * width
    first = jnp.concatenate([qkv_weight, out_weight], axis=0)
    first_rows = first.shape[0]
    first_parts = lax.all_gather(first, axes, axis=0, tiled=True)
    merge_padded = jnp.concatenate(
        [merge_weight, jnp.zeros((tile_rows - merge_rows, wide), merge_weight.dtype)], axis=0
    )
    merge_parts = lax.all_gather(merge_padded, axes, axis=0, tiled=True)
    devices = first_parts.shape[0] // first_rows
    group = 8
    blocks = first_parts.reshape(devices // group, group * first_rows, width)
    source = lax.broadcasted_iota(jnp.int32, (1, group * first_rows), 1)

    def selector(rows, offset):
        target = lax.broadcasted_iota(jnp.int32, (group * rows, 1), 0)
        wanted = (target // rows) * first_rows + offset + target % rows
        return (wanted == source).astype(first_parts.dtype)

    def pick(rows, offset):
        picked = jnp.einsum(
            "ij,bjk->bik", selector(rows, offset), blocks, preferred_element_type=jnp.float32
        )
        return picked.astype(first_parts.dtype).reshape(devices * rows, width)

    qkv_full = pick(qkv_rows, 0)
    out_full = pick(out_rows, qkv_rows)
    merge_full = merge_parts

    normed = layer_norm(patch_states, first_gain, first_shift).astype(jnp.bfloat16)
    joined_t = lax.dot_general(
        qkv_full, normed, (((1,), (1,)), ((), ())), preferred_element_type=jnp.float32
    )
    joined_t = (joined_t + qkv_bias[:, None]).astype(jnp.bfloat16)

    attended_t = attention(joined_t, segment_ids, 1024)

    projected_att = lax.dot_general(
        attended_t, out_full, (((0,), (1,)), ((), ())), preferred_element_type=jnp.float32
    )
    hidden = (patch_states.astype(jnp.float32) + projected_att + out_bias).astype(
        jnp.bfloat16
    )
    merged = (
        layer_norm(hidden, second_gain, second_shift)
        .astype(jnp.bfloat16)
        .reshape(tokens // 4, 4 * width)
    )
    projected_padded = lax.optimization_barrier(times_rows(merged, merge_full))
    bias_padded = jnp.pad(
        merge_bias.reshape(devices, merge_rows), ((0, 0), (0, tile_rows - merge_rows))
    ).reshape(-1)
    projected_padded = (projected_padded + bias_padded).astype(jnp.bfloat16)
    column = lax.broadcasted_iota(jnp.int32, (1, width), 1)
    padded_column = lax.broadcasted_iota(jnp.int32, (devices * tile_rows, 1), 0)
    keep = (
        padded_column == (column // merge_rows) * tile_rows + column % merge_rows
    ).astype(jnp.bfloat16)
    projected = jnp.dot(projected_padded, keep, preferred_element_type=jnp.float32).astype(
        jnp.bfloat16
    )

    fsdp_count = lax.axis_size("fsdp")
    dp_count = lax.axis_size("dp")
    count_dev = fsdp_count * dp_count
    row_count = tokens // 4
    capacity = 2 * (row_count // count_dev)
    matches = (dest_device[:, None] == jnp.arange(count_dev, dtype=jnp.int32)[None, :]).astype(
        jnp.int32
    )
    earlier = jnp.cumsum(matches, axis=0) - matches
    rank = jnp.sum(earlier * matches, axis=1)
    position = dest_device * capacity + rank
    place = (
        position[None, :] == jnp.arange(count_dev * capacity, dtype=jnp.int32)[:, None]
    ).astype(jnp.bfloat16)
    empty = jnp.sum(place, axis=1) == 0
    slot_sent = jnp.where(
        empty, row_count, jnp.sum(place.astype(jnp.int32) * dest_slot[None, :], axis=1)
    )
    got_slots = lax.all_to_all(
        slot_sent.reshape(count_dev, capacity), axes, split_axis=0, concat_axis=0, tiled=True
    ).reshape(-1)
    rows_out = jnp.dot(place, projected, preferred_element_type=jnp.float32).astype(jnp.bfloat16)
    got = lax.all_to_all(
        rows_out.reshape(count_dev, capacity, width), axes, split_axis=0, concat_axis=0, tiled=True
    ).reshape(count_dev * capacity, width)
    pick = (
        got_slots[None, :] == jnp.arange(row_count, dtype=jnp.int32)[:, None]
    ).astype(jnp.bfloat16)
    requests = jnp.dot(pick, got, preferred_element_type=jnp.float32).astype(jnp.bfloat16)
    return requests


def solution(mesh):
    in_specs = (
        P(("fsdp", "dp"), None),
        P(("fsdp", "dp")),
        P(),
        P(),
        P(("fsdp", "dp"), None),
        P(),
        P(("fsdp", "dp"), None),
        P(),
        P(),
        P(),
        P(("fsdp", "dp"), None),
        P(),
        P(("fsdp", "dp")),
        P(("fsdp", "dp")),
    )
    out_specs = P(("fsdp", "dp"), None)
    return jax.shard_map(
        per_device, mesh=mesh, in_specs=in_specs, out_specs=out_specs, check_vma=False
    )
```

```python
import functools
import math

import jax
import jax.numpy as jnp
from jax import lax
from jax.experimental import pallas as pl
from jax.experimental.pallas import tpu as pltpu
from jax.sharding import PartitionSpec as P

D = 1280
H = 16
HD = 80


EPSILON = 1e-06


def layer_norm(states, gain, shift):
    values = states.astype(jnp.float32)
    center = jnp.mean(values, axis=-1, keepdims=True)
    spread = jnp.mean(jnp.square(values - center), axis=-1, keepdims=True)
    return (values - center) * lax.rsqrt(spread + EPSILON) * gain + shift


def times_rows(left, piece):
    return lax.dot_general(
        left, piece, (((1,), (1,)), ((), ())), preferred_element_type=jnp.float32
    )


def attention_kernel(scale, q_ref, k_ref, v_ref, qid_ref, kid_ref, o_ref):
    q = q_ref[...]
    k = k_ref[...]
    v = v_ref[...]
    scores = lax.dot_general(
        q, k, (((0,), (0,)), ((), ())), preferred_element_type=jnp.float32
    )
    scores = scores * scale
    same = qid_ref[...] == kid_ref[...]
    masked = jnp.where(same, scores, -jnp.inf)
    top = jnp.max(masked, axis=-1, keepdims=True)
    expo = jnp.exp(masked - top)
    total = jnp.sum(expo, axis=-1, keepdims=True)
    probs = (expo / total).astype(jnp.bfloat16)
    out = lax.dot_general(
        v, probs, (((1,), (1,)), ((), ())), preferred_element_type=jnp.float32
    )
    o_ref[...] = out.astype(o_ref.dtype)


def attention(joined_t, segment_ids, block_q):
    tokens = joined_t.shape[1]
    scale = 1.0 / math.sqrt(HD)
    qid = segment_ids.reshape(tokens, 1)
    kid = segment_ids.reshape(1, tokens)
    flops = 4 * H * tokens * tokens * HD
    cost = pl.CostEstimate(
        flops=flops,
        transcendentals=H * tokens * tokens,
        bytes_accessed=joined_t.size * 2 + tokens * D * 2,
    )
    return pl.pallas_call(
        functools.partial(attention_kernel, scale),
        out_shape=jax.ShapeDtypeStruct((D, tokens), jnp.bfloat16),
        grid=(H, tokens // block_q),
        in_specs=[
            pl.BlockSpec((HD, block_q), lambda h, i: (h, i)),
            pl.BlockSpec((HD, tokens), lambda h, i: (H + h, 0)),
            pl.BlockSpec((HD, tokens), lambda h, i: (2 * H + h, 0)),
            pl.BlockSpec((block_q, 1), lambda h, i: (i, 0)),
            pl.BlockSpec((1, tokens), lambda h, i: (0, 0)),
        ],
        out_specs=pl.BlockSpec((HD, block_q), lambda h, i: (h, i)),
        cost_estimate=cost,
    )(joined_t, joined_t, joined_t, qid, kid)


def per_device(
    patch_states,
    segment_ids,
    first_gain,
    first_shift,
    qkv_weight,
    qkv_bias,
    out_weight,
    out_bias,
    second_gain,
    second_shift,
    merge_weight,
    merge_bias,
    dest_device,
    dest_slot,
):
    tokens = patch_states.shape[0]
    width = D
    axes = ("fsdp", "dp")

    qkv_rows = qkv_weight.shape[0]
    out_rows = out_weight.shape[0]
    merge_rows = merge_weight.shape[0]
    tile_rows = 16
    wide = 4 * width
    first = jnp.concatenate([qkv_weight, out_weight], axis=0)
    first_rows = first.shape[0]
    first_parts = lax.all_gather(first, axes, axis=0, tiled=True)
    merge_padded = jnp.concatenate(
        [merge_weight, jnp.zeros((tile_rows - merge_rows, wide), merge_weight.dtype)], axis=0
    )
    merge_parts = lax.all_gather(merge_padded, axes, axis=0, tiled=True)
    devices = first_parts.shape[0] // first_rows
    group = 8
    blocks = first_parts.reshape(devices // group, group * first_rows, width)
    source = lax.broadcasted_iota(jnp.int32, (1, group * first_rows), 1)

    def selector(rows, offset):
        target = lax.broadcasted_iota(jnp.int32, (group * rows, 1), 0)
        wanted = (target // rows) * first_rows + offset + target % rows
        return (wanted == source).astype(first_parts.dtype)

    def pick(rows, offset):
        picked = jnp.einsum(
            "ij,bjk->bik", selector(rows, offset), blocks, preferred_element_type=jnp.float32
        )
        return picked.astype(first_parts.dtype).reshape(devices * rows, width)

    qkv_full = pick(qkv_rows, 0)
    out_full = pick(out_rows, qkv_rows)
    merge_full = merge_parts

    normed = layer_norm(patch_states, first_gain, first_shift).astype(jnp.bfloat16)
    joined_t = lax.dot_general(
        qkv_full, normed, (((1,), (1,)), ((), ())), preferred_element_type=jnp.float32
    )
    joined_t = (joined_t + qkv_bias[:, None]).astype(jnp.bfloat16)

    attended_t = attention(joined_t, segment_ids, 1024)

    projected_att = lax.dot_general(
        attended_t, out_full, (((0,), (1,)), ((), ())), preferred_element_type=jnp.float32
    )
    hidden = (patch_states.astype(jnp.float32) + projected_att + out_bias).astype(
        jnp.bfloat16
    )
    merged = (
        layer_norm(hidden, second_gain, second_shift)
        .astype(jnp.bfloat16)
        .reshape(tokens // 4, 4 * width)
    )
    fsdp_count = lax.axis_size("fsdp")
    dp_count = lax.axis_size("dp")
    count_dev = fsdp_count * dp_count
    row_count = tokens // 4
    capacity = 2 * (row_count // count_dev)
    matches = (dest_device[:, None] == jnp.arange(count_dev, dtype=jnp.int32)[None, :]).astype(
        jnp.int32
    )
    earlier = jnp.cumsum(matches, axis=0) - matches
    rank = jnp.sum(earlier * matches, axis=1)
    position = dest_device * capacity + rank
    place = (
        position[None, :] == jnp.arange(count_dev * capacity, dtype=jnp.int32)[:, None]
    ).astype(jnp.bfloat16)
    empty = jnp.sum(place, axis=1) == 0
    slot_sent = jnp.where(
        empty, row_count, jnp.sum(place.astype(jnp.int32) * dest_slot[None, :], axis=1)
    )
    got_slots = lax.all_to_all(
        slot_sent.reshape(count_dev, capacity), axes, split_axis=0, concat_axis=0, tiled=True
    ).reshape(-1)
    halves = 2
    half_rows = devices * tile_rows // halves
    half_width = width // halves
    results = []
    for half in range(halves):
        padded = lax.optimization_barrier(
            times_rows(merged, merge_full[half * half_rows : (half + 1) * half_rows])
        )
        projected = padded.reshape(tokens // 4, devices // halves, tile_rows)[:, :, :merge_rows]
        projected = (
            projected.reshape(tokens // 4, half_width)
            + merge_bias[half * half_width : (half + 1) * half_width]
        ).astype(jnp.bfloat16)
        rows_out = jnp.dot(place, projected, preferred_element_type=jnp.float32).astype(
            jnp.bfloat16
        )
        got = lax.all_to_all(
            rows_out.reshape(count_dev, capacity, half_width),
            axes,
            split_axis=0,
            concat_axis=0,
            tiled=True,
        ).reshape(count_dev * capacity, half_width)
        results.append(got)
    got = jnp.concatenate(results, axis=1)
    pick = (
        got_slots[None, :] == jnp.arange(row_count, dtype=jnp.int32)[:, None]
    ).astype(jnp.bfloat16)
    requests = jnp.dot(pick, got, preferred_element_type=jnp.float32).astype(jnp.bfloat16)
    return requests


def solution(mesh):
    in_specs = (
        P(("fsdp", "dp"), None),
        P(("fsdp", "dp")),
        P(),
        P(),
        P(("fsdp", "dp"), None),
        P(),
        P(("fsdp", "dp"), None),
        P(),
        P(),
        P(),
        P(("fsdp", "dp"), None),
        P(),
        P(("fsdp", "dp")),
        P(("fsdp", "dp")),
    )
    out_specs = P(("fsdp", "dp"), None)
    return jax.shard_map(
        per_device, mesh=mesh, in_specs=in_specs, out_specs=out_specs, check_vma=False
    )
```

```python
import functools
import math

import jax
import jax.numpy as jnp
from jax import lax
from jax.experimental import pallas as pl
from jax.experimental.pallas import tpu as pltpu
from jax.sharding import PartitionSpec as P

D = 1280
H = 16
HD = 80


EPSILON = 1e-06


def layer_norm(states, gain, shift):
    values = states.astype(jnp.float32)
    center = jnp.mean(values, axis=-1, keepdims=True)
    spread = jnp.mean(jnp.square(values - center), axis=-1, keepdims=True)
    return (values - center) * lax.rsqrt(spread + EPSILON) * gain + shift


def times_rows(left, piece):
    return lax.dot_general(
        left, piece, (((1,), (1,)), ((), ())), preferred_element_type=jnp.float32
    )


def attention_kernel(scale, q_ref, k_ref, v_ref, qid_ref, kid_ref, o_ref):
    q = q_ref[...]
    k = k_ref[...]
    v = v_ref[...]
    scores = lax.dot_general(
        q, k, (((0,), (0,)), ((), ())), preferred_element_type=jnp.float32
    )
    scores = scores * scale
    same = qid_ref[...] == kid_ref[...]
    masked = jnp.where(same, scores, -jnp.inf)
    top = jnp.max(masked, axis=-1, keepdims=True)
    expo = jnp.exp(masked - top)
    total = jnp.sum(expo, axis=-1, keepdims=True)
    probs = (expo / total).astype(jnp.bfloat16)
    out = lax.dot_general(
        v, probs, (((1,), (1,)), ((), ())), preferred_element_type=jnp.float32
    )
    o_ref[...] = out.astype(o_ref.dtype)


def attention(joined_t, segment_ids, block_q):
    tokens = joined_t.shape[1]
    scale = 1.0 / math.sqrt(HD)
    qid = segment_ids.reshape(tokens, 1)
    kid = segment_ids.reshape(1, tokens)
    flops = 4 * H * tokens * tokens * HD
    cost = pl.CostEstimate(
        flops=flops,
        transcendentals=H * tokens * tokens,
        bytes_accessed=joined_t.size * 2 + tokens * D * 2,
    )
    return pl.pallas_call(
        functools.partial(attention_kernel, scale),
        out_shape=jax.ShapeDtypeStruct((D, tokens), jnp.bfloat16),
        grid=(H, tokens // block_q),
        in_specs=[
            pl.BlockSpec((HD, block_q), lambda h, i: (h, i)),
            pl.BlockSpec((HD, tokens), lambda h, i: (H + h, 0)),
            pl.BlockSpec((HD, tokens), lambda h, i: (2 * H + h, 0)),
            pl.BlockSpec((block_q, 1), lambda h, i: (i, 0)),
            pl.BlockSpec((1, tokens), lambda h, i: (0, 0)),
        ],
        out_specs=pl.BlockSpec((HD, block_q), lambda h, i: (h, i)),
        cost_estimate=cost,
    )(joined_t, joined_t, joined_t, qid, kid)


def per_device(
    patch_states,
    segment_ids,
    first_gain,
    first_shift,
    qkv_weight,
    qkv_bias,
    out_weight,
    out_bias,
    second_gain,
    second_shift,
    merge_weight,
    merge_bias,
    dest_device,
    dest_slot,
):
    tokens = patch_states.shape[0]
    width = D
    axes = ("fsdp", "dp")

    qkv_rows = qkv_weight.shape[0]
    out_rows = out_weight.shape[0]
    merge_rows = merge_weight.shape[0]
    tile_rows = 16
    wide = 4 * width
    first = jnp.concatenate([qkv_weight, out_weight], axis=0)
    first_rows = first.shape[0]
    first_parts = lax.all_gather(first, axes, axis=0, tiled=True)
    merge_padded = jnp.concatenate(
        [merge_weight, jnp.zeros((tile_rows - merge_rows, wide), merge_weight.dtype)], axis=0
    )
    merge_parts = lax.all_gather(merge_padded, axes, axis=0, tiled=True)
    devices = first_parts.shape[0] // first_rows
    group = 8
    blocks = first_parts.reshape(devices // group, group * first_rows, width)
    source = lax.broadcasted_iota(jnp.int32, (1, group * first_rows), 1)

    def selector(rows, offset):
        target = lax.broadcasted_iota(jnp.int32, (group * rows, 1), 0)
        wanted = (target // rows) * first_rows + offset + target % rows
        return (wanted == source).astype(first_parts.dtype)

    def pick(rows, offset):
        picked = jnp.einsum(
            "ij,bjk->bik", selector(rows, offset), blocks, preferred_element_type=jnp.float32
        )
        return picked.astype(first_parts.dtype).reshape(devices * rows, width)

    qkv_full = pick(qkv_rows, 0)
    out_full = pick(out_rows, qkv_rows)
    merge_full = merge_parts

    normed = layer_norm(patch_states, first_gain, first_shift).astype(jnp.bfloat16)
    joined_t = lax.dot_general(
        qkv_full, normed, (((1,), (1,)), ((), ())), preferred_element_type=jnp.float32
    )
    joined_t = (joined_t + qkv_bias[:, None]).astype(jnp.bfloat16)

    attended_t = attention(joined_t, segment_ids, 1024)

    projected_att = lax.dot_general(
        attended_t, out_full, (((0,), (1,)), ((), ())), preferred_element_type=jnp.float32
    )
    hidden = (patch_states.astype(jnp.float32) + projected_att + out_bias).astype(
        jnp.bfloat16
    )
    merged = (
        layer_norm(hidden, second_gain, second_shift)
        .astype(jnp.bfloat16)
        .reshape(tokens // 4, 4 * width)
    )
    projected_padded = lax.optimization_barrier(times_rows(merge_full, merged))
    projected_t = projected_padded.reshape(devices, tile_rows, tokens // 4)[:, :merge_rows]
    projected_t = (projected_t.reshape(width, tokens // 4) + merge_bias[:, None]).astype(
        jnp.bfloat16
    )

    fsdp_count = lax.axis_size("fsdp")
    dp_count = lax.axis_size("dp")
    count_dev = fsdp_count * dp_count
    row_count = tokens // 4
    capacity = 2 * (row_count // count_dev)
    matches = (dest_device[:, None] == jnp.arange(count_dev, dtype=jnp.int32)[None, :]).astype(
        jnp.int32
    )
    earlier = jnp.cumsum(matches, axis=0) - matches
    rank = jnp.sum(earlier * matches, axis=1)
    position = dest_device * capacity + rank
    place = (
        position[None, :] == jnp.arange(count_dev * capacity, dtype=jnp.int32)[:, None]
    ).astype(jnp.bfloat16)
    empty = jnp.sum(place, axis=1) == 0
    slot_sent = jnp.where(
        empty, row_count, jnp.sum(place.astype(jnp.int32) * dest_slot[None, :], axis=1)
    )
    got_slots = lax.all_to_all(
        slot_sent.reshape(count_dev, capacity), axes, split_axis=0, concat_axis=0, tiled=True
    ).reshape(-1)
    rows_out = times_rows(place, projected_t).astype(jnp.bfloat16)
    got = lax.all_to_all(
        rows_out.reshape(count_dev, capacity, width), axes, split_axis=0, concat_axis=0, tiled=True
    ).reshape(count_dev * capacity, width)
    pick = (
        got_slots[None, :] == jnp.arange(row_count, dtype=jnp.int32)[:, None]
    ).astype(jnp.bfloat16)
    requests = jnp.dot(pick, got, preferred_element_type=jnp.float32).astype(jnp.bfloat16)
    return requests


def solution(mesh):
    in_specs = (
        P(("fsdp", "dp"), None),
        P(("fsdp", "dp")),
        P(),
        P(),
        P(("fsdp", "dp"), None),
        P(),
        P(("fsdp", "dp"), None),
        P(),
        P(),
        P(),
        P(("fsdp", "dp"), None),
        P(),
        P(("fsdp", "dp")),
        P(("fsdp", "dp")),
    )
    out_specs = P(("fsdp", "dp"), None)
    return jax.shard_map(
        per_device, mesh=mesh, in_specs=in_specs, out_specs=out_specs, check_vma=False
    )
```
